32 devices in a mesh: mem: 8 (over z, y), head: 4 (over x, core).
Axes of the slice: x: 2, y: 2, z: 4, core: 2. Of those that a mesh axis runs over, the one named last changes fastest.
Arguments:
- queries: bfloat16 [4096, 2048], P('mem', 'head'), may hold values from -8 to 8
- local_keys: bfloat16 [4096, 2048], P('mem', 'head'), may hold values from -8 to 8
- local_values: bfloat16 [4096, 2048], P('mem', 'head'), may hold values from -8 to 8
- memory_keys: bfloat16 [128, 32, 2048], P('mem', None, 'head'), may hold values from -8 to 8
- memory_values: bfloat16 [128, 32, 2048], P('mem', None, 'head'), may hold values from -8 to 8
- retrieval: int32 [8, 32], replicated, may hold values from 0 to 127, as said below
- gate_logit: float32 [16], P('head'), may hold values from -4 to 4
- dropout_keep: int32 [4096, 2048], P('mem', 'head'), may hold values 0 or 1
- out_weight: bfloat16 [2048, 2048], P('head'), may hold values from -0.125 to 0.125
- cotangent: bfloat16 [4096, 2048], P('mem', 'head'), may hold values from -6 to 6
Outputs:
- layer_out: bfloat16 [4096, 2048], P('mem', 'head')
- grad_queries: bfloat16 [4096, 2048], P('mem', 'head')
- grad_keys: bfloat16 [4096, 2048], P('mem', 'head')
- grad_values: bfloat16 [4096, 2048], P('mem', 'head')
- grad_memory_keys: bfloat16 [128, 32, 2048], P('mem', None, 'head')
- grad_memory_values: bfloat16 [128, 32, 2048], P('mem', None, 'head')
The draws below stay inside these ranges and needn't reach their ends.
Inputs may be any that keep to these rules, and one draw needn't show every extreme that they name: `retrieval`: block i lies on shard i // 16. Rows d * 1 to (d + 1) - 1 belong to index d of mem; together they name 32 distinct blocks, at most 8 of them on any one shard, and in every draw one shard receives exactly 8 from the rows of every index.
All inputs are finite; a program needn't handle non-finite values. No bound on the sum of `dropout_keep` on one device may be relied on, other than what follows from the above.
Results may differ from the reference program's by a relative error of at most 0.0079.
Values may be sent and summed in bfloat16 or wider, within the bound.
No kernel may reach another device: no remote copies, remote signals or barrier semaphores. Data moves between devices by JAX's collectives and lax.ppermute only.
A program may use at most 128 MiB of HBM per device.

```python
import jax
import jax.numpy as jnp
from jax import lax

D = 2048
HEADS = 16
HEAD_DIM = 128
QBLK = 512
BLK = 32
TOPB = 32
MBLK_DEV = 16
HD = 2048
TOKENS = 4096
QB_DEV = 1
QBLOCKS = 8
MEM_BLOCKS = 128
CAP = 8
N_MEM = 8


def drawn_rows(key, first, shape):
    return jnp.clip(jax.random.normal(jax.random.fold_in(key, first), shape, jnp.float32), -6.0, 6.0)


def draw_queries(key, part):
    drawn = drawn_rows(key, 1, (TOKENS, HD))
    return drawn.astype(jnp.bfloat16)


def draw_local_keys(key, part):
    drawn = drawn_rows(key, 3, (TOKENS, HD))
    return drawn.astype(jnp.bfloat16)


def draw_local_values(key, part):
    drawn = drawn_rows(key, 5, (TOKENS, HD))
    return drawn.astype(jnp.bfloat16)


def draw_memory_keys(key, part):
    drawn = drawn_rows(key, 7, (MEM_BLOCKS, BLK, HD))
    return drawn.astype(jnp.bfloat16)


def draw_memory_values(key, part):
    drawn = drawn_rows(key, 9, (MEM_BLOCKS, BLK, HD))
    return drawn.astype(jnp.bfloat16)


def device_requests(device_key, hot_owner):
    request_count = QB_DEV * TOPB
    others = jax.random.permutation(jax.random.fold_in(device_key, 1), N_MEM - 1).astype(jnp.int32)
    owner_order = jnp.concatenate([hot_owner[None], (hot_owner + 1 + others) % N_MEM]).astype(jnp.int32)
    doubled = jax.random.randint(jax.random.fold_in(device_key, 2), (), 1, N_MEM // 2 + 1).astype(jnp.int32)
    position = jnp.arange(request_count, dtype=jnp.int32)
    full_part = doubled * CAP
    rest = position - full_part
    remaining_owners = N_MEM - doubled
    owner_slot = jnp.where(position < full_part, position // CAP, doubled + rest % remaining_owners)
    occurrence = jnp.where(position < full_part, position % CAP, rest // remaining_owners)
    owner_ids = owner_order[owner_slot]
    offsets = jax.random.randint(jax.random.fold_in(device_key, 3), (N_MEM,), 0, MBLK_DEV).astype(jnp.int32)
    block_ids = owner_ids * MBLK_DEV + (offsets[owner_ids] + occurrence) % MBLK_DEV
    shuffle = jax.random.permutation(jax.random.fold_in(device_key, 4), request_count)
    return block_ids[shuffle]


def draw_retrieval(key, part):
    hot_owner = jax.random.randint(jax.random.fold_in(key, 11), (), 0, N_MEM).astype(jnp.int32)
    device_keys = jax.random.split(jax.random.fold_in(key, 14), N_MEM)
    block_ids = jax.vmap(device_requests, in_axes=(0, None))(device_keys, hot_owner)
    return block_ids.reshape(QBLOCKS, TOPB).astype(jnp.int32)


def plant(values, stream_key, least, largest):
    place = [jax.random.randint(jax.random.fold_in(stream_key, axis), (), 0, length) for axis, length in enumerate(values.shape)]
    main_axis = values.shape.index(max(values.shape))
    next_to = place[:main_axis] + [(place[main_axis] + 1) % values.shape[main_axis]] + place[main_axis + 1:]
    return values.at[tuple(place)].set(least).at[tuple(next_to)].set(largest)


def level_of(own_key, dims, pieces, least, largest):
    factor_of = 1.0
    for axis_at, shards_of in pieces:
        heights = jax.random.uniform(jax.random.fold_in(jax.random.fold_in(own_key, 6), axis_at), (shards_of,), jnp.float32, least / len(pieces), largest / len(pieces))
        factor_of = factor_of * jnp.repeat(jnp.exp(heights), dims[axis_at] // shards_of).reshape((-1,) + (1,) * (len(dims) - 1 - axis_at))
    return factor_of


def bell_draw(rng, shape, scale, limit, cuts=(), kind=jnp.bfloat16):
    values = scale * jax.random.normal(rng, shape, jnp.float32)
    if cuts:
        values = values * level_of(rng, shape, cuts, -0.22, 0.18)
    return jnp.clip(values, -limit, limit).astype(kind)


def setup_inputs(seed: int = 0) -> dict:
    seeds = jax.random.split(jax.random.key(seed), 11)
    queries = draw_queries(jax.random.fold_in(seeds[10], 71), 0)
    local_keys = draw_local_keys(jax.random.fold_in(seeds[10], 71), 0)
    local_values = draw_local_values(jax.random.fold_in(seeds[10], 71), 0)
    memory_keys = draw_memory_keys(jax.random.fold_in(seeds[10], 71), 0)
    memory_values = draw_memory_values(jax.random.fold_in(seeds[10], 71), 0)
    retrieval = draw_retrieval(jax.random.fold_in(seeds[10], 71), 0)
    gate_logit = bell_draw(seeds[6], (HEADS,), 1.5, 4.0, ((0, 4),), jnp.float32)
    dropout_keep = plant((jax.random.randint(seeds[7], (TOKENS, HD), 0, 10) < 9).astype(jnp.int32), jax.random.fold_in(seeds[7], 1), 0, 1)
    out_weight = bell_draw(seeds[8], (HD, D), HD ** -0.5, 0.125, ((0, 4),))
    cotangent = bell_draw(seeds[9], (TOKENS, D), 1.0, 6.0, ((0, 8), (1, 4)))
    return dict(queries=queries, local_keys=local_keys, local_values=local_values, memory_keys=memory_keys, memory_values=memory_values, retrieval=retrieval, gate_logit=gate_logit, dropout_keep=dropout_keep, out_weight=out_weight, cotangent=cotangent)


keep_scale = 1.0 / 0.9


def rounded(array):
    return lax.optimization_barrier(array.astype(jnp.bfloat16)).astype(jnp.float32)


def matmul(left, right):
    return jnp.dot(left, right, preferred_element_type=jnp.float32)


def head_pass(query_rows, key_local, value_local, key_memory, value_memory, gate_value, keep_mask, grad_dropped):
    score_scale = HEAD_DIM ** -0.5
    position = jnp.arange(QBLK, dtype=jnp.int32)
    allowed = position[None, :] <= position[:, None]

    def weights_of(keyset, causal):
        scores = matmul(query_rows, keyset.T) * score_scale
        if causal:
            scores = jnp.where(allowed, scores, -jnp.inf)
        return jnp.exp(scores - jnp.max(scores, axis=1, keepdims=True))

    def forward(keyset, valueset, causal):
        weights = weights_of(keyset, causal)
        row_total = jnp.sum(weights, axis=1, keepdims=True)
        return weights, row_total, matmul(rounded(weights), valueset) / row_total

    def backward(weights, row_total, mixed_out, keyset, valueset, grad_mixed):
        probabilities = weights / row_total
        delta_rows = jnp.sum(grad_mixed * mixed_out, axis=1, keepdims=True)
        grad_low = rounded(grad_mixed)
        grad_probs = matmul(grad_low, valueset.T)
        grad_scores = rounded(probabilities * (grad_probs - delta_rows) * score_scale)
        grad_query = matmul(grad_scores, keyset)
        grad_keyset = matmul(grad_scores.T, query_rows)
        grad_valueset = matmul(rounded(probabilities).T, grad_low)
        return grad_query, grad_keyset, grad_valueset

    weights_loc, total_loc, mixed_loc = forward(key_local, value_local, True)
    weights_mem, total_mem, mixed_mem = forward(key_memory, value_memory, False)
    attended = gate_value * mixed_mem + (1.0 - gate_value) * mixed_loc
    dropped = (attended * keep_mask * keep_scale).astype(jnp.bfloat16)
    grad_attended = grad_dropped * keep_mask * keep_scale
    query_mem, keyset_mem, valueset_mem = backward(weights_mem, total_mem, mixed_mem, key_memory, value_memory, gate_value * grad_attended)
    query_loc, keyset_loc, valueset_loc = backward(weights_loc, total_loc, mixed_loc, key_local, value_local, (1.0 - gate_value) * grad_attended)
    return (dropped, (query_mem + query_loc).astype(jnp.bfloat16), keyset_loc.astype(jnp.bfloat16),
            valueset_loc.astype(jnp.bfloat16), keyset_mem.astype(jnp.bfloat16), valueset_mem.astype(jnp.bfloat16))


def reference(queries, local_keys, local_values, memory_keys, memory_values, retrieval, gate_logit, dropout_keep, out_weight, cotangent):
    gate_values = 1.0 / (1.0 + jnp.exp(-gate_logit))
    head_map = jax.vmap(head_pass, in_axes=(1, 1, 1, 1, 1, 0, 1, 1), out_axes=1)

    def split_heads(array):
        return array.astype(jnp.float32).reshape(array.shape[0], HEADS, HEAD_DIM)

    def block_step(accumulated, block_index):
        start = block_index * QBLK

        def rows_of(array):
            return lax.dynamic_slice_in_dim(array, start, QBLK, 0)

        chosen = retrieval[block_index]
        key_memory = split_heads(memory_keys[chosen].reshape(TOPB * BLK, HD))
        value_memory = split_heads(memory_values[chosen].reshape(TOPB * BLK, HD))
        grad_dropped = jnp.dot(rows_of(cotangent), out_weight.T, preferred_element_type=jnp.float32).reshape(QBLK, HEADS, HEAD_DIM)
        dropped, grad_query, grad_key, grad_value, part_keys, part_values = head_map(
            split_heads(rows_of(queries)), split_heads(rows_of(local_keys)), split_heads(rows_of(local_values)),
            key_memory, value_memory, gate_values, split_heads(rows_of(dropout_keep)), grad_dropped)
        layer_rows = jnp.dot(dropped.reshape(QBLK, HD), out_weight, preferred_element_type=jnp.float32).astype(jnp.bfloat16)
        part_keys = lax.optimization_barrier(part_keys.reshape(TOPB, BLK, HD)).astype(jnp.float32)
        part_values = lax.optimization_barrier(part_values.reshape(TOPB, BLK, HD)).astype(jnp.float32)
        sum_keys = accumulated[0].at[chosen].add(part_keys)
        sum_values = accumulated[1].at[chosen].add(part_values)
        return (sum_keys, sum_values), (layer_rows, grad_query.reshape(QBLK, HD), grad_key.reshape(QBLK, HD), grad_value.reshape(QBLK, HD))

    zeros_start = jnp.zeros((MEM_BLOCKS, BLK, HD), jnp.float32)
    totals, stacked = lax.scan(block_step, (zeros_start, zeros_start), jnp.arange(QBLOCKS, dtype=jnp.int32))
    layer_out = stacked[0].reshape(TOKENS, D)
    grad_queries = stacked[1].reshape(TOKENS, HD)
    grad_keys = stacked[2].reshape(TOKENS, HD)
    grad_values = stacked[3].reshape(TOKENS, HD)
    return (layer_out, grad_queries, grad_keys, grad_values,
            totals[0].astype(jnp.bfloat16), totals[1].astype(jnp.bfloat16))
```

```python
import jax
import jax.numpy as jnp
from jax import lax
from jax.sharding import PartitionSpec as P

QBLK = 512


keep_scale = 1.0 / 0.9


def mm(spec, left, right):
    return jnp.einsum(spec, left, right, preferred_element_type=jnp.float32)


def branch(query_rows, keyset, valueset, grad_mixed, causal, score_scale):
    scores = mm("thd,khd->htk", query_rows, keyset) * score_scale
    if causal:
        row_iota = lax.broadcasted_iota(jnp.int32, scores.shape, 1)
        col_iota = lax.broadcasted_iota(jnp.int32, scores.shape, 2)
        scores = jnp.where(col_iota <= row_iota, scores, -jnp.inf)
    weights = jnp.exp(scores - jnp.max(scores, axis=2, keepdims=True))
    row_total = jnp.sum(weights, axis=2, keepdims=True)
    mixed_out = mm("htk,khd->htd", weights.astype(jnp.bfloat16), valueset) / row_total
    return weights, row_total, mixed_out


def branch_grads(query_rows, keyset, valueset, weights, row_total, mixed_out, grad_mixed, score_scale):
    probabilities = weights / row_total
    delta_rows = jnp.sum(grad_mixed * mixed_out, axis=2, keepdims=True)
    grad_low = grad_mixed.astype(jnp.bfloat16)
    grad_probs = mm("htd,khd->htk", grad_low, valueset)
    grad_scores = (probabilities * (grad_probs - delta_rows) * score_scale).astype(jnp.bfloat16)
    grad_query = mm("htk,khd->thd", grad_scores, keyset)
    grad_keyset = mm("htk,thd->khd", grad_scores, query_rows)
    grad_valueset = mm("htk,htd->khd", probabilities.astype(jnp.bfloat16), grad_low)
    return grad_query, grad_keyset, grad_valueset


def per_device(
    queries,
    local_keys,
    local_values,
    memory_keys,
    memory_values,
    retrieval,
    gate_logit,
    dropout_keep,
    out_weight,
    cotangent,
):
    mem_count = lax.axis_size("mem")
    mem_index = lax.axis_index("mem")
    tok_rows, feature_cols = queries.shape
    heads_here = gate_logit.shape[0]
    head_dim = feature_cols // heads_here
    score_scale = head_dim ** (-0.5)
    blocks_here = memory_keys.shape[0]
    block_len = memory_keys.shape[1]
    query_blocks = tok_rows // QBLK
    top_blocks = retrieval.shape[1]
    request_count = query_blocks * top_blocks
    capacity = 2 * request_count // mem_count
    slot_count = mem_count * capacity
    owner_ids = retrieval // blocks_here
    local_ids = retrieval % blocks_here
    earlier_mask = lax.broadcasted_iota(
        jnp.int32, (request_count, request_count), 0
    ) < lax.broadcasted_iota(jnp.int32, (request_count, request_count), 1)
    same_owner = owner_ids[:, :, None] == owner_ids[:, None, :]
    owner_rank = jnp.sum((same_owner & earlier_mask[None]).astype(jnp.int32), axis=1)
    request_owner = lax.dynamic_index_in_dim(owner_ids, mem_index, 0, keepdims=False)
    request_rank = lax.dynamic_index_in_dim(owner_rank, mem_index, 0, keepdims=False)
    request_slot = request_owner * capacity + request_rank
    slot_iota = lax.broadcasted_iota(jnp.int32, (request_count, slot_count), 1)
    pick_table = (request_slot[:, None] == slot_iota).astype(jnp.bfloat16)
    cap_iota = lax.broadcasted_iota(jnp.int32, (mem_count, request_count, capacity), 2)
    wanted = (owner_ids[:, :, None] == mem_index) & (owner_rank[:, :, None] == cap_iota)
    send_local = jnp.sum(wanted.astype(jnp.int32) * (local_ids[:, :, None] + 1), axis=1) - 1
    block_iota = lax.broadcasted_iota(jnp.int32, (slot_count, blocks_here), 1)
    serve_table = (send_local.reshape(slot_count, 1) == block_iota).astype(jnp.bfloat16)

    both = jnp.concatenate([memory_keys, memory_values], axis=2)
    entries2 = block_len * 2 * feature_cols
    served = jnp.dot(
        serve_table, both.reshape(blocks_here, entries2), preferred_element_type=jnp.float32
    ).astype(jnp.bfloat16)
    fetched = lax.all_to_all(
        served.reshape(mem_count, capacity, block_len, 2 * feature_cols),
        "mem", split_axis=0, concat_axis=0, tiled=True,
    )
    chosen = jnp.dot(
        pick_table, fetched.reshape(slot_count, entries2), preferred_element_type=jnp.float32
    ).astype(jnp.bfloat16).reshape(top_blocks * block_len, 2 * feature_cols)
    mem_keyset = chosen[:, :feature_cols].reshape(-1, heads_here, head_dim)
    mem_valueset = chosen[:, feature_cols:].reshape(-1, heads_here, head_dim)

    gate_values = 1.0 / (1.0 + jnp.exp(-gate_logit))
    gate_col = gate_values[None, :, None]
    keep_mask = dropout_keep.astype(jnp.float32)

    query_rows = queries.reshape(tok_rows, heads_here, head_dim)
    key_rows = local_keys.reshape(tok_rows, heads_here, head_dim)
    value_rows = local_values.reshape(tok_rows, heads_here, head_dim)

    cotangent_full = lax.all_gather(cotangent, "head", axis=1, tiled=True)
    grad_attended = lax.dot_general(
        cotangent_full, out_weight, (((1,), (1,)), ((), ())), preferred_element_type=jnp.float32
    ) * keep_mask * keep_scale
    grad_heads = grad_attended.reshape(tok_rows, heads_here, head_dim)
    grad_mem = (gate_col * grad_heads).transpose(1, 0, 2)
    grad_loc = ((1.0 - gate_col) * grad_heads).transpose(1, 0, 2)

    w_loc, l_loc, o_loc = branch(query_rows, key_rows, value_rows, grad_loc, True, score_scale)
    q_loc, k_loc, v_loc = branch_grads(
        query_rows, key_rows, value_rows, w_loc, l_loc, o_loc, grad_loc, score_scale
    )
    w_mem, l_mem, o_mem = branch(query_rows, mem_keyset, mem_valueset, grad_mem, False, score_scale)
    q_mem, k_mem, v_mem = branch_grads(
        query_rows, mem_keyset, mem_valueset, w_mem, l_mem, o_mem, grad_mem, score_scale
    )

    attended = (gate_col * o_mem.transpose(1, 0, 2) + (1.0 - gate_col) * o_loc.transpose(1, 0, 2))
    dropped = (attended.reshape(tok_rows, feature_cols) * keep_mask * keep_scale).astype(jnp.bfloat16)
    partial_out = jnp.dot(dropped, out_weight, preferred_element_type=jnp.float32)
    layer_out = lax.psum_scatter(partial_out, "head", scatter_dimension=1, tiled=True).astype(
        jnp.bfloat16
    )

    grad_queries = (q_mem + q_loc).astype(jnp.bfloat16).reshape(tok_rows, feature_cols)
    grad_keys = k_loc.astype(jnp.bfloat16).reshape(tok_rows, feature_cols)
    grad_values = v_loc.astype(jnp.bfloat16).reshape(tok_rows, feature_cols)

    parts = jnp.concatenate(
        [
            k_mem.astype(jnp.bfloat16).reshape(top_blocks, block_len, feature_cols),
            v_mem.astype(jnp.bfloat16).reshape(top_blocks, block_len, feature_cols),
        ],
        axis=2,
    ).reshape(top_blocks, entries2)
    send = lax.dot_general(
        pick_table, parts, (((0,), (0,)), ((), ())), preferred_element_type=jnp.float32
    ).astype(jnp.bfloat16)
    returned = lax.all_to_all(
        send.reshape(mem_count, capacity, block_len, 2 * feature_cols),
        "mem", split_axis=0, concat_axis=0, tiled=True,
    )
    summed = lax.dot_general(
        serve_table, returned.reshape(slot_count, entries2), (((0,), (0,)), ((), ())),
        preferred_element_type=jnp.float32,
    ).astype(jnp.bfloat16).reshape(blocks_here, block_len, 2 * feature_cols)
    return (
        layer_out,
        grad_queries,
        grad_keys,
        grad_values,
        summed[:, :, :feature_cols],
        summed[:, :, feature_cols:],
    )


def solution(mesh):
    placed = (
        P("mem", "head"),
        P("mem", "head"),
        P("mem", "head"),
        P("mem", None, "head"),
        P("mem", None, "head"),
        P(),
        P("head"),
        P("mem", "head"),
        P("head", None),
        P("mem", "head"),
    )
    return jax.shard_map(
        per_device,
        mesh=mesh,
        in_specs=placed,
        out_specs=(
            P("mem", "head"),
            P("mem", "head"),
            P("mem", "head"),
            P("mem", "head"),
            P("mem", None, "head"),
            P("mem", None, "head"),
        ),
        check_vma=False,
    )
```

```python
import jax
import jax.numpy as jnp
from jax import lax
from jax.sharding import PartitionSpec as P

QBLK = 512
CHUNKS = 2


keep_scale = 1.0 / 0.9


def mm(spec, left, right):
    return jnp.einsum(spec, left, right, preferred_element_type=jnp.float32)


def branch(query_rows, keyset, valueset, grad_mixed, causal, score_scale):
    scores = mm("thd,khd->htk", query_rows, keyset) * score_scale
    if causal:
        row_iota = lax.broadcasted_iota(jnp.int32, scores.shape, 1)
        col_iota = lax.broadcasted_iota(jnp.int32, scores.shape, 2)
        scores = jnp.where(col_iota <= row_iota, scores, -jnp.inf)
    weights = jnp.exp(scores - jnp.max(scores, axis=2, keepdims=True))
    row_total = jnp.sum(weights, axis=2, keepdims=True)
    mixed_out = mm("htk,khd->htd", weights.astype(jnp.bfloat16), valueset) / row_total
    return weights, row_total, mixed_out


def branch_grads(query_rows, keyset, valueset, weights, row_total, mixed_out, grad_mixed, score_scale):
    probabilities = weights / row_total
    delta_rows = jnp.sum(grad_mixed * mixed_out, axis=2, keepdims=True)
    grad_low = grad_mixed.astype(jnp.bfloat16)
    grad_probs = mm("htd,khd->htk", grad_low, valueset)
    grad_scores = (probabilities * (grad_probs - delta_rows) * score_scale).astype(jnp.bfloat16)
    grad_query = mm("htk,khd->thd", grad_scores, keyset)
    grad_keyset = mm("htk,thd->khd", grad_scores, query_rows)
    grad_valueset = mm("htk,htd->khd", probabilities.astype(jnp.bfloat16), grad_low)
    return grad_query, grad_keyset, grad_valueset


def per_device(
    queries,
    local_keys,
    local_values,
    memory_keys,
    memory_values,
    retrieval,
    gate_logit,
    dropout_keep,
    out_weight,
    cotangent,
):
    mem_count = lax.axis_size("mem")
    mem_index = lax.axis_index("mem")
    tok_rows, feature_cols = queries.shape
    heads_here = gate_logit.shape[0]
    head_dim = feature_cols // heads_here
    score_scale = head_dim ** (-0.5)
    blocks_here = memory_keys.shape[0]
    block_len = memory_keys.shape[1]
    query_blocks = tok_rows // QBLK
    top_blocks = retrieval.shape[1]
    request_count = query_blocks * top_blocks
    capacity = 2 * request_count // mem_count
    slot_count = mem_count * capacity
    owner_ids = retrieval // blocks_here
    local_ids = retrieval % blocks_here
    earlier_mask = lax.broadcasted_iota(
        jnp.int32, (request_count, request_count), 0
    ) < lax.broadcasted_iota(jnp.int32, (request_count, request_count), 1)
    same_owner = owner_ids[:, :, None] == owner_ids[:, None, :]
    owner_rank = jnp.sum((same_owner & earlier_mask[None]).astype(jnp.int32), axis=1)
    request_owner = lax.dynamic_index_in_dim(owner_ids, mem_index, 0, keepdims=False)
    request_rank = lax.dynamic_index_in_dim(owner_rank, mem_index, 0, keepdims=False)
    request_slot = request_owner * capacity + request_rank
    slot_iota = lax.broadcasted_iota(jnp.int32, (request_count, slot_count), 1)
    pick_table = (request_slot[:, None] == slot_iota).astype(jnp.bfloat16)
    cap_iota = lax.broadcasted_iota(jnp.int32, (mem_count, request_count, capacity), 2)
    wanted = (owner_ids[:, :, None] == mem_index) & (owner_rank[:, :, None] == cap_iota)
    send_local = jnp.sum(wanted.astype(jnp.int32) * (local_ids[:, :, None] + 1), axis=1) - 1
    block_iota = lax.broadcasted_iota(jnp.int32, (slot_count, blocks_here), 1)
    serve_table = (send_local.reshape(slot_count, 1) == block_iota).astype(jnp.bfloat16)

    gate_values = 1.0 / (1.0 + jnp.exp(-gate_logit))
    gate_col = gate_values[None, :, None]
    keep_mask = dropout_keep.astype(jnp.float32)

    query_rows = queries.reshape(tok_rows, heads_here, head_dim)
    key_rows = local_keys.reshape(tok_rows, heads_here, head_dim)
    value_rows = local_values.reshape(tok_rows, heads_here, head_dim)

    chunk_heads = heads_here // CHUNKS if heads_here % CHUNKS == 0 else heads_here
    chunk_count = heads_here // chunk_heads
    chunk_cols = chunk_heads * head_dim
    entries2 = block_len * 2 * chunk_cols

    def fetch(chunk):
        cols = slice(chunk * chunk_cols, (chunk + 1) * chunk_cols)
        both = jnp.concatenate([memory_keys[:, :, cols], memory_values[:, :, cols]], axis=2)
        served = jnp.dot(
            serve_table, both.reshape(blocks_here, entries2), preferred_element_type=jnp.float32
        ).astype(jnp.bfloat16)
        return lax.all_to_all(
            served.reshape(mem_count, capacity, block_len, 2 * chunk_cols),
            "mem", split_axis=0, concat_axis=0, tiled=True,
        )

    fetched = [fetch(0)]

    cotangent_full = lax.all_gather(cotangent, "head", axis=1, tiled=True)
    grad_attended = lax.dot_general(
        cotangent_full, out_weight, (((1,), (1,)), ((), ())), preferred_element_type=jnp.float32
    ) * keep_mask * keep_scale
    grad_heads = grad_attended.reshape(tok_rows, heads_here, head_dim)
    grad_mem = (gate_col * grad_heads).transpose(1, 0, 2)
    grad_loc = ((1.0 - gate_col) * grad_heads).transpose(1, 0, 2)

    w_loc, l_loc, o_loc = branch(query_rows, key_rows, value_rows, grad_loc, True, score_scale)
    q_loc, k_loc, v_loc = branch_grads(
        query_rows, key_rows, value_rows, w_loc, l_loc, o_loc, grad_loc, score_scale
    )

    if chunk_count > 1:
        memory_keys, memory_values, o_loc, q_loc, k_loc, v_loc, grad_mem = lax.optimization_barrier(
            (memory_keys, memory_values, o_loc, q_loc, k_loc, v_loc, grad_mem)
        )
    o_mem_parts, q_mem_parts, summed_parts = [], [], []
    for chunk in range(chunk_count):
        if chunk + 1 < chunk_count:
            fetched.append(fetch(chunk + 1))
        heads = slice(chunk * chunk_heads, (chunk + 1) * chunk_heads)
        chosen = jnp.dot(
            pick_table, fetched[chunk].reshape(slot_count, entries2),
            preferred_element_type=jnp.float32,
        ).astype(jnp.bfloat16).reshape(top_blocks * block_len, 2 * chunk_cols)
        mem_keyset = chosen[:, :chunk_cols].reshape(-1, chunk_heads, head_dim)
        mem_valueset = chosen[:, chunk_cols:].reshape(-1, chunk_heads, head_dim)
        q_chunk = query_rows[:, heads]
        g_chunk = grad_mem[heads]
        w_mem, l_mem, o_mem = branch(q_chunk, mem_keyset, mem_valueset, g_chunk, False, score_scale)
        q_mem, k_mem, v_mem = branch_grads(
            q_chunk, mem_keyset, mem_valueset, w_mem, l_mem, o_mem, g_chunk, score_scale
        )
        o_mem_parts.append(o_mem)
        q_mem_parts.append(q_mem)
        parts = jnp.concatenate(
            [
                k_mem.astype(jnp.bfloat16).reshape(top_blocks, block_len, chunk_cols),
                v_mem.astype(jnp.bfloat16).reshape(top_blocks, block_len, chunk_cols),
            ],
            axis=2,
        ).reshape(top_blocks, entries2)
        send = lax.dot_general(
            pick_table, parts, (((0,), (0,)), ((), ())), preferred_element_type=jnp.float32
        ).astype(jnp.bfloat16)
        returned = lax.all_to_all(
            send.reshape(mem_count, capacity, block_len, 2 * chunk_cols),
            "mem", split_axis=0, concat_axis=0, tiled=True,
        )
        summed_parts.append(lax.dot_general(
            serve_table, returned.reshape(slot_count, entries2), (((0,), (0,)), ((), ())),
            preferred_element_type=jnp.float32,
        ).astype(jnp.bfloat16).reshape(blocks_here, block_len, 2 * chunk_cols))

    o_mem = jnp.concatenate(o_mem_parts, axis=0)
    q_mem = jnp.concatenate(q_mem_parts, axis=1)
    attended = (gate_col * o_mem.transpose(1, 0, 2) + (1.0 - gate_col) * o_loc.transpose(1, 0, 2))
    dropped = (attended.reshape(tok_rows, feature_cols) * keep_mask * keep_scale).astype(jnp.bfloat16)
    partial_out = jnp.dot(dropped, out_weight, preferred_element_type=jnp.float32)
    layer_out = lax.psum_scatter(partial_out, "head", scatter_dimension=1, tiled=True).astype(
        jnp.bfloat16
    )

    grad_queries = (q_mem + q_loc).astype(jnp.bfloat16).reshape(tok_rows, feature_cols)
    grad_keys = k_loc.astype(jnp.bfloat16).reshape(tok_rows, feature_cols)
    grad_values = v_loc.astype(jnp.bfloat16).reshape(tok_rows, feature_cols)
    grad_memory_keys = jnp.concatenate([s[:, :, :chunk_cols] for s in summed_parts], axis=2)
    grad_memory_values = jnp.concatenate([s[:, :, chunk_cols:] for s in summed_parts], axis=2)
    return (
        layer_out,
        grad_queries,
        grad_keys,
        grad_values,
        grad_memory_keys,
        grad_memory_values,
    )


def solution(mesh):
    placed = (
        P("mem", "head"),
        P("mem", "head"),
        P("mem", "head"),
        P("mem", None, "head"),
        P("mem", None, "head"),
        P(),
        P("head"),
        P("mem", "head"),
        P("head", None),
        P("mem", "head"),
    )
    return jax.shard_map(
        per_device,
        mesh=mesh,
        in_specs=placed,
        out_specs=(
            P("mem", "head"),
            P("mem", "head"),
            P("mem", "head"),
            P("mem", "head"),
            P("mem", None, "head"),
            P("mem", None, "head"),
        ),
        check_vma=False,
    )
```

```python
import functools

import jax
import jax.numpy as jnp
from jax import lax
from jax.experimental import pallas as pl
from jax.experimental.pallas import tpu as pltpu
from jax.sharding import PartitionSpec as P

QBLK = 512
CHUNKS = 2


keep_scale = 1.0 / 0.9


def _branch_kernel(q_ref, k_ref, v_ref, g_ref, o_ref, dq_ref, dk_ref, dv_ref, *, causal, score_scale):
    q = q_ref[...]
    k = k_ref[...]
    v = v_ref[...]
    g = g_ref[...]
    scores = lax.dot_general(
        q, k, (((1,), (1,)), ((), ())), preferred_element_type=jnp.float32
    ) * score_scale
    if causal:
        row = lax.broadcasted_iota(jnp.int32, scores.shape, 0)
        col = lax.broadcasted_iota(jnp.int32, scores.shape, 1)
        scores = jnp.where(col <= row, scores, -jnp.inf)
    weights = jnp.exp(scores - jnp.max(scores, axis=1, keepdims=True))
    total = jnp.sum(weights, axis=1, keepdims=True)
    mixed = jnp.dot(weights.astype(jnp.bfloat16), v, preferred_element_type=jnp.float32) / total
    o_ref[...] = mixed
    probs = weights / total
    delta = jnp.sum(g * mixed, axis=1, keepdims=True)
    g_low = g.astype(jnp.bfloat16)
    grad_probs = lax.dot_general(
        g_low, v, (((1,), (1,)), ((), ())), preferred_element_type=jnp.float32
    )
    ds = (probs * (grad_probs - delta) * score_scale).astype(jnp.bfloat16)
    dq_ref[...] = jnp.dot(ds, k, preferred_element_type=jnp.float32)
    dk_ref[...] = lax.dot_general(
        ds, q, (((0,), (0,)), ((), ())), preferred_element_type=jnp.float32
    ).astype(dk_ref.dtype)
    dv_ref[...] = lax.dot_general(
        probs.astype(jnp.bfloat16), g_low, (((0,), (0,)), ((), ())),
        preferred_element_type=jnp.float32,
    ).astype(dv_ref.dtype)


def attention_branch(q, g, k, v, heads, head_dim, causal, q_off=0, k_off=0, v_off=0):
    rows = q.shape[0]
    keys = k.shape[0]
    cols = heads * head_dim
    kernel = functools.partial(_branch_kernel, causal=causal, score_scale=head_dim ** (-0.5))

    def spec(length, offset):
        return pl.BlockSpec((length, head_dim), lambda h: (0, h + offset))

    out_row = pl.BlockSpec((rows, head_dim), lambda h: (0, h))
    out_key = pl.BlockSpec((keys, head_dim), lambda h: (0, h))
    return pl.pallas_call(
        kernel,
        grid=(heads,),
        in_specs=[spec(rows, q_off), spec(keys, k_off), spec(keys, v_off), spec(rows, q_off)],
        out_specs=[out_row, out_row, out_key, out_key],
        out_shape=[
            jax.ShapeDtypeStruct((rows, cols), jnp.float32),
            jax.ShapeDtypeStruct((rows, cols), jnp.float32),
            jax.ShapeDtypeStruct((keys, cols), jnp.bfloat16),
            jax.ShapeDtypeStruct((keys, cols), jnp.bfloat16),
        ],
        compiler_params=pltpu.CompilerParams(vmem_limit_bytes=48 * 1024 * 1024),
        cost_estimate=pl.CostEstimate(
            flops=12 * rows * keys * head_dim * heads,
            transcendentals=rows * keys * heads,
            bytes_accessed=rows * cols * 14 + keys * cols * 8,
        ),
    )(q, k, v, g)


def per_device(
    queries,
    local_keys,
    local_values,
    memory_keys,
    memory_values,
    retrieval,
    gate_logit,
    dropout_keep,
    out_weight,
    cotangent,
):
    mem_count = lax.axis_size("mem")
    mem_index = lax.axis_index("mem")
    tok_rows, feature_cols = queries.shape
    heads_here = gate_logit.shape[0]
    head_dim = feature_cols // heads_here
    score_scale = head_dim ** (-0.5)
    blocks_here = memory_keys.shape[0]
    block_len = memory_keys.shape[1]
    query_blocks = tok_rows // QBLK
    top_blocks = retrieval.shape[1]
    request_count = query_blocks * top_blocks
    capacity = 2 * request_count // mem_count
    slot_count = mem_count * capacity
    owner_ids = retrieval // blocks_here
    local_ids = retrieval % blocks_here
    earlier_mask = lax.broadcasted_iota(
        jnp.int32, (request_count, request_count), 0
    ) < lax.broadcasted_iota(jnp.int32, (request_count, request_count), 1)
    same_owner = owner_ids[:, :, None] == owner_ids[:, None, :]
    owner_rank = jnp.sum((same_owner & earlier_mask[None]).astype(jnp.int32), axis=1)
    request_owner = lax.dynamic_index_in_dim(owner_ids, mem_index, 0, keepdims=False)
    request_rank = lax.dynamic_index_in_dim(owner_rank, mem_index, 0, keepdims=False)
    request_slot = request_owner * capacity + request_rank
    slot_iota = lax.broadcasted_iota(jnp.int32, (request_count, slot_count), 1)
    pick_table = (request_slot[:, None] == slot_iota).astype(jnp.bfloat16)
    cap_iota = lax.broadcasted_iota(jnp.int32, (mem_count, request_count, capacity), 2)
    wanted = (owner_ids[:, :, None] == mem_index) & (owner_rank[:, :, None] == cap_iota)
    send_local = jnp.sum(wanted.astype(jnp.int32) * (local_ids[:, :, None] + 1), axis=1) - 1
    block_iota = lax.broadcasted_iota(jnp.int32, (slot_count, blocks_here), 1)
    serve_table = (send_local.reshape(slot_count, 1) == block_iota).astype(jnp.bfloat16)

    gate_values = 1.0 / (1.0 + jnp.exp(-gate_logit))
    gate_cols = jnp.repeat(gate_values, head_dim)[None, :]
    keep_mask = dropout_keep.astype(jnp.float32)

    chunk_heads = heads_here // CHUNKS if heads_here % CHUNKS == 0 else heads_here
    chunk_count = heads_here // chunk_heads
    chunk_cols = chunk_heads * head_dim
    entries2 = block_len * 2 * chunk_cols

    def fetch(chunk):
        cols = slice(chunk * chunk_cols, (chunk + 1) * chunk_cols)
        both = jnp.concatenate([memory_keys[:, :, cols], memory_values[:, :, cols]], axis=2)
        served = jnp.dot(
            serve_table, both.reshape(blocks_here, entries2), preferred_element_type=jnp.float32
        ).astype(jnp.bfloat16)
        return lax.all_to_all(
            served.reshape(mem_count, capacity, block_len, 2 * chunk_cols),
            "mem", split_axis=0, concat_axis=0, tiled=True,
        )

    fetched = [fetch(0)]

    cotangent_full = lax.all_gather(cotangent, "head", axis=1, tiled=True)
    grad_attended = lax.dot_general(
        cotangent_full, out_weight, (((1,), (1,)), ((), ())), preferred_element_type=jnp.float32
    ) * keep_mask * keep_scale
    grad_mem = gate_cols * grad_attended
    grad_loc = (1.0 - gate_cols) * grad_attended

    o_loc, q_loc, k_loc, v_loc = attention_branch(
        queries, grad_loc, local_keys, local_values, heads_here, head_dim, True
    )

    if chunk_count > 1:
        memory_keys, memory_values, o_loc, q_loc, k_loc, v_loc, grad_mem = lax.optimization_barrier(
            (memory_keys, memory_values, o_loc, q_loc, k_loc, v_loc, grad_mem)
        )
    o_mem_parts, q_mem_parts, summed_parts = [], [], []
    for chunk in range(chunk_count):
        if chunk + 1 < chunk_count:
            fetched.append(fetch(chunk + 1))
        chosen = jnp.dot(
            pick_table, fetched[chunk].reshape(slot_count, entries2),
            preferred_element_type=jnp.float32,
        ).astype(jnp.bfloat16).reshape(top_blocks * block_len, 2 * chunk_cols)
        o_mem, q_mem, k_mem, v_mem = attention_branch(
            queries, grad_mem, chosen, chosen, chunk_heads, head_dim, False,
            q_off=chunk * chunk_heads, k_off=0, v_off=chunk_heads,
        )
        o_mem_parts.append(o_mem)
        q_mem_parts.append(q_mem)
        parts = jnp.concatenate([k_mem, v_mem], axis=1).reshape(top_blocks, entries2)
        send = lax.dot_general(
            pick_table, parts, (((0,), (0,)), ((), ())), preferred_element_type=jnp.float32
        ).astype(jnp.bfloat16)
        returned = lax.all_to_all(
            send.reshape(mem_count, capacity, block_len, 2 * chunk_cols),
            "mem", split_axis=0, concat_axis=0, tiled=True,
        )
        summed_parts.append(lax.dot_general(
            serve_table, returned.reshape(slot_count, entries2), (((0,), (0,)), ((), ())),
            preferred_element_type=jnp.float32,
        ).astype(jnp.bfloat16).reshape(blocks_here, block_len, 2 * chunk_cols))

    o_mem = jnp.concatenate(o_mem_parts, axis=1)
    q_mem = jnp.concatenate(q_mem_parts, axis=1)
    attended = gate_cols * o_mem + (1.0 - gate_cols) * o_loc
    dropped = (attended * keep_mask * keep_scale).astype(jnp.bfloat16)
    partial_out = jnp.dot(dropped, out_weight, preferred_element_type=jnp.float32)
    layer_out = lax.psum_scatter(partial_out, "head", scatter_dimension=1, tiled=True).astype(
        jnp.bfloat16
    )

    grad_queries = (q_mem + q_loc).astype(jnp.bfloat16)
    grad_keys = k_loc
    grad_values = v_loc
    grad_memory_keys = jnp.concatenate([s[:, :, :chunk_cols] for s in summed_parts], axis=2)
    grad_memory_values = jnp.concatenate([s[:, :, chunk_cols:] for s in summed_parts], axis=2)
    return (
        layer_out,
        grad_queries,
        grad_keys,
        grad_values,
        grad_memory_keys,
        grad_memory_values,
    )


def solution(mesh):
    placed = (
        P("mem", "head"),
        P("mem", "head"),
        P("mem", "head"),
        P("mem", None, "head"),
        P("mem", None, "head"),
        P(),
        P("head"),
        P("mem", "head"),
        P("head", None),
        P("mem", "head"),
    )
    return jax.shard_map(
        per_device,
        mesh=mesh,
        in_specs=placed,
        out_specs=(
            P("mem", "head"),
            P("mem", "head"),
            P("mem", "head"),
            P("mem", "head"),
            P("mem", None, "head"),
            P("mem", None, "head"),
        ),
        check_vma=False,
    )
```

```python
import functools

import jax
import jax.numpy as jnp
from jax import lax
from jax.experimental import pallas as pl
from jax.experimental.pallas import tpu as pltpu
from jax.sharding import PartitionSpec as P


QBLK = 512
CHUNKS = 2


keep_scale = 1.0 / 0.9


def _branch_kernel(q_ref, k_ref, v_ref, g_ref, o_ref, dq_ref, dk_ref, dv_ref, *, causal, score_scale):
    q = q_ref[...]
    k = k_ref[...]
    v = v_ref[...]
    g = g_ref[...]
    scores = lax.dot_general(
        q, k, (((1,), (1,)), ((), ())), preferred_element_type=jnp.float32
    ) * score_scale
    if causal:
        row = lax.broadcasted_iota(jnp.int32, scores.shape, 0)
        col = lax.broadcasted_iota(jnp.int32, scores.shape, 1)
        scores = jnp.where(col <= row, scores, -jnp.inf)
    weights = jnp.exp(scores - jnp.max(scores, axis=1, keepdims=True))
    total = jnp.sum(weights, axis=1, keepdims=True)
    mixed = jnp.dot(weights.astype(jnp.bfloat16), v, preferred_element_type=jnp.float32) / total
    o_ref[...] = mixed
    probs = weights / total
    delta = jnp.sum(g * mixed, axis=1, keepdims=True)
    g_low = g.astype(jnp.bfloat16)
    grad_probs = lax.dot_general(
        g_low, v, (((1,), (1,)), ((), ())), preferred_element_type=jnp.float32
    )
    ds = (probs * (grad_probs - delta) * score_scale).astype(jnp.bfloat16)
    dq_ref[...] = jnp.dot(ds, k, preferred_element_type=jnp.float32)
    dk_ref[...] = lax.dot_general(
        ds, q, (((0,), (0,)), ((), ())), preferred_element_type=jnp.float32
    ).astype(dk_ref.dtype)
    dv_ref[...] = lax.dot_general(
        probs.astype(jnp.bfloat16), g_low, (((0,), (0,)), ((), ())),
        preferred_element_type=jnp.float32,
    ).astype(dv_ref.dtype)


def attention_branch(q, g, k, v, heads, head_dim, causal, q_off=0, k_off=0, v_off=0):
    rows = q.shape[0]
    keys = k.shape[0]
    cols = heads * head_dim
    kernel = functools.partial(_branch_kernel, causal=causal, score_scale=head_dim ** (-0.5))

    def spec(length, offset):
        return pl.BlockSpec((length, head_dim), lambda h: (0, h + offset))

    out_row = pl.BlockSpec((rows, head_dim), lambda h: (0, h))
    out_key = pl.BlockSpec((keys, head_dim), lambda h: (0, h))
    return pl.pallas_call(
        kernel,
        grid=(heads,),
        in_specs=[spec(rows, q_off), spec(keys, k_off), spec(keys, v_off), spec(rows, q_off)],
        out_specs=[out_row, out_row, out_key, out_key],
        out_shape=[
            jax.ShapeDtypeStruct((rows, cols), jnp.float32),
            jax.ShapeDtypeStruct((rows, cols), jnp.float32),
            jax.ShapeDtypeStruct((keys, cols), jnp.bfloat16),
            jax.ShapeDtypeStruct((keys, cols), jnp.bfloat16),
        ],
        compiler_params=pltpu.CompilerParams(vmem_limit_bytes=48 * 1024 * 1024),
        cost_estimate=pl.CostEstimate(
            flops=12 * rows * keys * head_dim * heads,
            transcendentals=rows * keys * heads,
            bytes_accessed=rows * cols * 14 + keys * cols * 8,
        ),
    )(q, k, v, g)


def per_device(
    queries,
    local_keys,
    local_values,
    memory_keys,
    memory_values,
    retrieval,
    gate_logit,
    dropout_keep,
    out_weight,
    cotangent,
):
    mem_count = lax.axis_size("mem")
    mem_index = lax.axis_index("mem")
    tok_rows, feature_cols = queries.shape
    heads_here = gate_logit.shape[0]
    head_dim = feature_cols // heads_here
    blocks_here = memory_keys.shape[0]
    block_len = memory_keys.shape[1]
    query_blocks = tok_rows // QBLK
    top_blocks = retrieval.shape[1]
    request_count = query_blocks * top_blocks
    capacity = 2 * request_count // mem_count
    slot_count = mem_count * capacity
    owner_ids = retrieval // blocks_here
    local_ids = retrieval % blocks_here
    earlier_mask = lax.broadcasted_iota(
        jnp.int32, (request_count, request_count), 0
    ) < lax.broadcasted_iota(jnp.int32, (request_count, request_count), 1)
    same_owner = owner_ids[:, :, None] == owner_ids[:, None, :]
    owner_rank = jnp.sum((same_owner & earlier_mask[None]).astype(jnp.int32), axis=1)
    request_owner = lax.dynamic_index_in_dim(owner_ids, mem_index, 0, keepdims=False)
    request_rank = lax.dynamic_index_in_dim(owner_rank, mem_index, 0, keepdims=False)
    request_slot = ((mem_index - request_owner) % mem_count) * capacity + request_rank
    slot_iota = lax.broadcasted_iota(jnp.int32, (request_count, slot_count), 1)
    pick_table = (request_slot[:, None] == slot_iota).astype(jnp.bfloat16)
    cap_iota = lax.broadcasted_iota(jnp.int32, (mem_count, request_count, capacity), 2)
    wanted = (owner_ids[:, :, None] == mem_index) & (owner_rank[:, :, None] == cap_iota)
    send_local = jnp.sum(wanted.astype(jnp.int32) * (local_ids[:, :, None] + 1), axis=1) - 1
    send_local = jnp.roll(send_local, -mem_index, axis=0)
    block_iota = lax.broadcasted_iota(jnp.int32, (slot_count, blocks_here), 1)
    serve_table = (send_local.reshape(slot_count, 1) == block_iota).astype(jnp.bfloat16)

    gate_values = 1.0 / (1.0 + jnp.exp(-gate_logit))
    gate_cols = jnp.repeat(gate_values, head_dim)[None, :]
    keep_mask = dropout_keep.astype(jnp.float32)

    chunk_heads = heads_here // CHUNKS if heads_here % CHUNKS == 0 else heads_here
    chunk_count = heads_here // chunk_heads
    chunk_cols = chunk_heads * head_dim
    entries2 = block_len * 2 * chunk_cols

    def exchange(buffer, sign):
        pieces = [buffer[0]]
        for shift in range(1, mem_count):
            pairs = [(i, (i + sign * shift) % mem_count) for i in range(mem_count)]
            pieces.append(lax.ppermute(buffer[shift], "mem", pairs))
        return jnp.stack(pieces)

    def fetch(chunk):
        cols = slice(chunk * chunk_cols, (chunk + 1) * chunk_cols)
        both = jnp.concatenate([memory_keys[:, :, cols], memory_values[:, :, cols]], axis=2)
        served = jnp.dot(
            serve_table, both.reshape(blocks_here, entries2), preferred_element_type=jnp.float32
        ).astype(jnp.bfloat16)
        return exchange(served.reshape(mem_count, capacity, block_len, 2 * chunk_cols), 1)

    fetched = [fetch(0)]

    cotangent_full = lax.all_gather(cotangent, "head", axis=1, tiled=True)
    grad_attended = lax.dot_general(
        cotangent_full, out_weight, (((1,), (1,)), ((), ())), preferred_element_type=jnp.float32
    ) * keep_mask * keep_scale
    grad_mem = gate_cols * grad_attended
    grad_loc = (1.0 - gate_cols) * grad_attended

    o_loc, q_loc, k_loc, v_loc = attention_branch(
        queries, grad_loc, local_keys, local_values, heads_here, head_dim, True
    )

    if chunk_count > 1:
        memory_keys, memory_values, o_loc, q_loc, k_loc, v_loc, grad_mem = lax.optimization_barrier(
            (memory_keys, memory_values, o_loc, q_loc, k_loc, v_loc, grad_mem)
        )
    o_mem_parts, q_mem_parts, summed_parts = [], [], []
    for chunk in range(chunk_count):
        if chunk + 1 < chunk_count:
            fetched.append(fetch(chunk + 1))
        chosen = jnp.dot(
            pick_table, fetched[chunk].reshape(slot_count, entries2),
            preferred_element_type=jnp.float32,
        ).astype(jnp.bfloat16).reshape(top_blocks * block_len, 2 * chunk_cols)
        o_mem, q_mem, k_mem, v_mem = attention_branch(
            queries, grad_mem, chosen, chosen, chunk_heads, head_dim, False,
            q_off=chunk * chunk_heads, k_off=0, v_off=chunk_heads,
        )
        o_mem_parts.append(o_mem)
        q_mem_parts.append(q_mem)
        parts = jnp.concatenate([k_mem, v_mem], axis=1).reshape(top_blocks, entries2)
        send = lax.dot_general(
            pick_table, parts, (((0,), (0,)), ((), ())), preferred_element_type=jnp.float32
        ).astype(jnp.bfloat16)
        if chunk + 1 < chunk_count:
            send, fetched[chunk + 1] = lax.optimization_barrier((send, fetched[chunk + 1]))
        returned = exchange(send.reshape(mem_count, capacity, block_len, 2 * chunk_cols), -1)
        summed_parts.append(lax.dot_general(
            serve_table, returned.reshape(slot_count, entries2), (((0,), (0,)), ((), ())),
            preferred_element_type=jnp.float32,
        ).astype(jnp.bfloat16).reshape(blocks_here, block_len, 2 * chunk_cols))

    o_mem = jnp.concatenate(o_mem_parts, axis=1)
    q_mem = jnp.concatenate(q_mem_parts, axis=1)
    attended = gate_cols * o_mem + (1.0 - gate_cols) * o_loc
    dropped = (attended * keep_mask * keep_scale).astype(jnp.bfloat16)
    partial_out = jnp.dot(dropped, out_weight, preferred_element_type=jnp.float32)
    layer_out = lax.psum_scatter(partial_out, "head", scatter_dimension=1, tiled=True).astype(
        jnp.bfloat16
    )

    grad_queries = (q_mem + q_loc).astype(jnp.bfloat16)
    grad_keys = k_loc
    grad_values = v_loc
    grad_memory_keys = jnp.concatenate([s[:, :, :chunk_cols] for s in summed_parts], axis=2)
    grad_memory_values = jnp.concatenate([s[:, :, chunk_cols:] for s in summed_parts], axis=2)
    return (
        layer_out,
        grad_queries,
        grad_keys,
        grad_values,
        grad_memory_keys,
        grad_memory_values,
    )


def solution(mesh):
    placed = (
        P("mem", "head"),
        P("mem", "head"),
        P("mem", "head"),
        P("mem", None, "head"),
        P("mem", None, "head"),
        P(),
        P("head"),
        P("mem", "head"),
        P("head", None),
        P("mem", "head"),
    )
    return jax.shard_map(
        per_device,
        mesh=mesh,
        in_specs=placed,
        out_specs=(
            P("mem", "head"),
            P("mem", "head"),
            P("mem", "head"),
            P("mem", "head"),
            P("mem", None, "head"),
            P("mem", None, "head"),
        ),
        check_vma=False,
    )
```

```python
import functools

import jax
import jax.numpy as jnp
from jax import lax
from jax.experimental import pallas as pl
from jax.experimental.pallas import tpu as pltpu
from jax.sharding import PartitionSpec as P


QBLK = 512
CHUNKS = 2


keep_scale = 1.0 / 0.9


def _branch_kernel(q_ref, k_ref, v_ref, g_ref, o_ref, dq_ref, dk_ref, dv_ref, *, causal, score_scale):
    q = q_ref[...]
    k = k_ref[...]
    v = v_ref[...]
    g = g_ref[...]
    scores = lax.dot_general(
        q, k, (((1,), (1,)), ((), ())), preferred_element_type=jnp.float32
    ) * score_scale
    if causal:
        row = lax.broadcasted_iota(jnp.int32, scores.shape, 0)
        col = lax.broadcasted_iota(jnp.int32, scores.shape, 1)
        scores = jnp.where(col <= row, scores, -jnp.inf)
    weights = jnp.exp(scores - jnp.max(scores, axis=1, keepdims=True))
    total = jnp.sum(weights, axis=1, keepdims=True)
    mixed = jnp.dot(weights.astype(jnp.bfloat16), v, preferred_element_type=jnp.float32) / total
    o_ref[...] = mixed
    probs = weights / total
    delta = jnp.sum(g * mixed, axis=1, keepdims=True)
    g_low = g.astype(jnp.bfloat16)
    grad_probs = lax.dot_general(
        g_low, v, (((1,), (1,)), ((), ())), preferred_element_type=jnp.float32
    )
    ds = (probs * (grad_probs - delta) * score_scale).astype(jnp.bfloat16)
    dq_ref[...] = jnp.dot(ds, k, preferred_element_type=jnp.float32)
    dk_ref[...] = lax.dot_general(
        ds, q, (((0,), (0,)), ((), ())), preferred_element_type=jnp.float32
    ).astype(dk_ref.dtype)
    dv_ref[...] = lax.dot_general(
        probs.astype(jnp.bfloat16), g_low, (((0,), (0,)), ((), ())),
        preferred_element_type=jnp.float32,
    ).astype(dv_ref.dtype)


def attention_branch(q, g, k, v, heads, head_dim, causal, q_off=0, k_off=0, v_off=0):
    rows = q.shape[0]
    keys = k.shape[0]
    cols = heads * head_dim
    kernel = functools.partial(_branch_kernel, causal=causal, score_scale=head_dim ** (-0.5))

    def spec(length, offset):
        return pl.BlockSpec((length, head_dim), lambda h: (0, h + offset))

    out_row = pl.BlockSpec((rows, head_dim), lambda h: (0, h))
    out_key = pl.BlockSpec((keys, head_dim), lambda h: (0, h))
    return pl.pallas_call(
        kernel,
        grid=(heads,),
        in_specs=[spec(rows, q_off), spec(keys, k_off), spec(keys, v_off), spec(rows, q_off)],
        out_specs=[out_row, out_row, out_key, out_key],
        out_shape=[
            jax.ShapeDtypeStruct((rows, cols), jnp.float32),
            jax.ShapeDtypeStruct((rows, cols), jnp.float32),
            jax.ShapeDtypeStruct((keys, cols), jnp.bfloat16),
            jax.ShapeDtypeStruct((keys, cols), jnp.bfloat16),
        ],
        compiler_params=pltpu.CompilerParams(vmem_limit_bytes=48 * 1024 * 1024),
        cost_estimate=pl.CostEstimate(
            flops=12 * rows * keys * head_dim * heads,
            transcendentals=rows * keys * heads,
            bytes_accessed=rows * cols * 14 + keys * cols * 8,
        ),
    )(q, k, v, g)


def per_device(
    queries,
    local_keys,
    local_values,
    memory_keys,
    memory_values,
    retrieval,
    gate_logit,
    dropout_keep,
    out_weight,
    cotangent,
):
    mem_count = lax.axis_size("mem")
    mem_index = lax.axis_index("mem")
    tok_rows, feature_cols = queries.shape
    heads_here = gate_logit.shape[0]
    head_dim = feature_cols // heads_here
    blocks_here = memory_keys.shape[0]
    block_len = memory_keys.shape[1]
    query_blocks = tok_rows // QBLK
    top_blocks = retrieval.shape[1]
    request_count = query_blocks * top_blocks
    capacity = 2 * request_count // mem_count
    slot_count = mem_count * capacity
    owner_ids = retrieval // blocks_here
    local_ids = retrieval % blocks_here
    earlier_mask = lax.broadcasted_iota(
        jnp.int32, (request_count, request_count), 0
    ) < lax.broadcasted_iota(jnp.int32, (request_count, request_count), 1)
    same_owner = owner_ids[:, :, None] == owner_ids[:, None, :]
    owner_rank = jnp.sum((same_owner & earlier_mask[None]).astype(jnp.int32), axis=1)
    request_owner = lax.dynamic_index_in_dim(owner_ids, mem_index, 0, keepdims=False)
    request_rank = lax.dynamic_index_in_dim(owner_rank, mem_index, 0, keepdims=False)
    request_slot = ((mem_index - request_owner) % mem_count) * capacity + request_rank
    slot_iota = lax.broadcasted_iota(jnp.int32, (request_count, slot_count), 1)
    pick_table = (request_slot[:, None] == slot_iota).astype(jnp.bfloat16)
    cap_iota = lax.broadcasted_iota(jnp.int32, (mem_count, request_count, capacity), 2)
    wanted = (owner_ids[:, :, None] == mem_index) & (owner_rank[:, :, None] == cap_iota)
    send_local = jnp.sum(wanted.astype(jnp.int32) * (local_ids[:, :, None] + 1), axis=1) - 1
    send_local = jnp.roll(send_local, -mem_index, axis=0)
    block_iota = lax.broadcasted_iota(jnp.int32, (slot_count, blocks_here), 1)
    serve_table = (send_local.reshape(slot_count, 1) == block_iota).astype(jnp.bfloat16)

    gate_values = 1.0 / (1.0 + jnp.exp(-gate_logit))
    gate_cols = jnp.repeat(gate_values, head_dim)[None, :]
    keep_mask = dropout_keep.astype(jnp.float32)

    chunk_heads = heads_here // CHUNKS if heads_here % CHUNKS == 0 else heads_here
    chunk_count = heads_here // chunk_heads
    chunk_cols = chunk_heads * head_dim
    entries2 = block_len * 2 * chunk_cols

    def exchange(buffer, sign):
        pieces = [buffer[0]]
        for shift in range(1, mem_count):
            pairs = [(i, (i + sign * shift) % mem_count) for i in range(mem_count)]
            pieces.append(lax.ppermute(buffer[shift], "mem", pairs))
        return pieces

    def gather_slots(table, pieces):
        total = None
        for shift, piece in enumerate(pieces):
            part = lax.dot_general(
                table[shift * capacity:(shift + 1) * capacity], piece.reshape(capacity, entries2),
                (((0,), (0,)), ((), ())), preferred_element_type=jnp.float32,
            )
            total = part if total is None else total + part
        return total.astype(jnp.bfloat16)

    def fetch(chunk):
        cols = slice(chunk * chunk_cols, (chunk + 1) * chunk_cols)
        both = jnp.concatenate([memory_keys[:, :, cols], memory_values[:, :, cols]], axis=2)
        served = jnp.dot(
            serve_table, both.reshape(blocks_here, entries2), preferred_element_type=jnp.float32
        ).astype(jnp.bfloat16)
        return exchange(served.reshape(mem_count, capacity, block_len, 2 * chunk_cols), 1)

    fetched = [fetch(0)]

    head_count = lax.axis_size("head")
    head_index = lax.axis_index("head")

    def weight_cols(owner):
        return lax.dynamic_slice_in_dim(out_weight, owner * feature_cols, feature_cols, axis=1)

    grad_proj = None
    for shift in range(head_count):
        if shift == 0:
            piece = cotangent
        else:
            pairs = [(i, (i + shift) % head_count) for i in range(head_count)]
            piece = lax.ppermute(cotangent, "head", pairs)
        owner = (head_index - shift) % head_count
        part = lax.dot_general(
            piece, weight_cols(owner), (((1,), (1,)), ((), ())), preferred_element_type=jnp.float32
        )
        grad_proj = part if grad_proj is None else grad_proj + part
    grad_attended = grad_proj * keep_mask * keep_scale
    grad_mem = gate_cols * grad_attended
    grad_loc = (1.0 - gate_cols) * grad_attended

    o_loc, q_loc, k_loc, v_loc = attention_branch(
        queries, grad_loc, local_keys, local_values, heads_here, head_dim, True
    )

    if chunk_count > 1:
        memory_keys, memory_values, o_loc, q_loc, k_loc, v_loc, grad_mem = lax.optimization_barrier(
            (memory_keys, memory_values, o_loc, q_loc, k_loc, v_loc, grad_mem)
        )
    o_mem_parts, q_mem_parts, summed_parts = [], [], []
    for chunk in range(chunk_count):
        if chunk + 1 < chunk_count:
            fetched.append(fetch(chunk + 1))
        chosen = gather_slots(pick_table.T, fetched[chunk]).reshape(
            top_blocks * block_len, 2 * chunk_cols
        )
        o_mem, q_mem, k_mem, v_mem = attention_branch(
            queries, grad_mem, chosen, chosen, chunk_heads, head_dim, False,
            q_off=chunk * chunk_heads, k_off=0, v_off=chunk_heads,
        )
        o_mem_parts.append(o_mem)
        q_mem_parts.append(q_mem)
        parts = jnp.concatenate([k_mem, v_mem], axis=1).reshape(top_blocks, entries2)
        send = lax.dot_general(
            pick_table, parts, (((0,), (0,)), ((), ())), preferred_element_type=jnp.float32
        ).astype(jnp.bfloat16)
        if chunk + 1 < chunk_count:
            send, fetched[chunk + 1] = lax.optimization_barrier((send, fetched[chunk + 1]))
        returned = exchange(send.reshape(mem_count, capacity, block_len, 2 * chunk_cols), -1)
        summed_parts.append(
            gather_slots(serve_table, returned).reshape(blocks_here, block_len, 2 * chunk_cols)
        )

    o_mem = jnp.concatenate(o_mem_parts, axis=1)
    q_mem = jnp.concatenate(q_mem_parts, axis=1)
    attended = gate_cols * o_mem + (1.0 - gate_cols) * o_loc
    dropped = (attended * keep_mask * keep_scale).astype(jnp.bfloat16)
    out_sum = None
    for shift in range(head_count):
        target = (head_index + shift) % head_count
        part = jnp.dot(dropped, weight_cols(target), preferred_element_type=jnp.float32)
        if shift:
            pairs = [(i, (i + shift) % head_count) for i in range(head_count)]
            part = lax.ppermute(part, "head", pairs)
        out_sum = part if out_sum is None else out_sum + part
    layer_out = out_sum.astype(jnp.bfloat16)

    grad_queries = (q_mem + q_loc).astype(jnp.bfloat16)
    grad_keys = k_loc
    grad_values = v_loc
    grad_memory_keys = jnp.concatenate([s[:, :, :chunk_cols] for s in summed_parts], axis=2)
    grad_memory_values = jnp.concatenate([s[:, :, chunk_cols:] for s in summed_parts], axis=2)
    return (
        layer_out,
        grad_queries,
        grad_keys,
        grad_values,
        grad_memory_keys,
        grad_memory_values,
    )


def solution(mesh):
    placed = (
        P("mem", "head"),
        P("mem", "head"),
        P("mem", "head"),
        P("mem", None, "head"),
        P("mem", None, "head"),
        P(),
        P("head"),
        P("mem", "head"),
        P("head", None),
        P("mem", "head"),
    )
    return jax.shard_map(
        per_device,
        mesh=mesh,
        in_specs=placed,
        out_specs=(
            P("mem", "head"),
            P("mem", "head"),
            P("mem", "head"),
            P("mem", "head"),
            P("mem", None, "head"),
            P("mem", None, "head"),
        ),
        check_vma=False,
    )
```

```python
import functools

import jax
import jax.numpy as jnp
from jax import lax
from jax.experimental import pallas as pl
from jax.experimental.pallas import tpu as pltpu
from jax.sharding import PartitionSpec as P


QBLK = 512
CHUNKS = 2


keep_scale = 1.0 / 0.9


def _branch_kernel(q_ref, k_ref, v_ref, g_ref, o_ref, dq_ref, dk_ref, dv_ref, *, causal, score_scale):
    q = q_ref[...]
    k = k_ref[...]
    v = v_ref[...]
    g = g_ref[...]
    scores = lax.dot_general(
        q, k, (((1,), (1,)), ((), ())), preferred_element_type=jnp.float32
    ) * score_scale
    if causal:
        row = lax.broadcasted_iota(jnp.int32, scores.shape, 0)
        col = lax.broadcasted_iota(jnp.int32, scores.shape, 1)
        scores = jnp.where(col <= row, scores, -jnp.inf)
    weights = jnp.exp(scores - jnp.max(scores, axis=1, keepdims=True))
    total = jnp.sum(weights, axis=1, keepdims=True)
    mixed = jnp.dot(weights.astype(jnp.bfloat16), v, preferred_element_type=jnp.float32) / total
    o_ref[...] = mixed
    probs = weights / total
    delta = jnp.sum(g * mixed, axis=1, keepdims=True)
    g_low = g.astype(jnp.bfloat16)
    grad_probs = lax.dot_general(
        g_low, v, (((1,), (1,)), ((), ())), preferred_element_type=jnp.float32
    )
    ds = (probs * (grad_probs - delta) * score_scale).astype(jnp.bfloat16)
    dq_ref[...] = jnp.dot(ds, k, preferred_element_type=jnp.float32)
    dk_ref[...] = lax.dot_general(
        ds, q, (((0,), (0,)), ((), ())), preferred_element_type=jnp.float32
    ).astype(dk_ref.dtype)
    dv_ref[...] = lax.dot_general(
        probs.astype(jnp.bfloat16), g_low, (((0,), (0,)), ((), ())),
        preferred_element_type=jnp.float32,
    ).astype(dv_ref.dtype)


def attention_branch(q, g, k, v, heads, head_dim, causal, q_off=0, k_off=0, v_off=0):
    rows = q.shape[0]
    keys = k.shape[0]
    cols = heads * head_dim
    kernel = functools.partial(_branch_kernel, causal=causal, score_scale=head_dim ** (-0.5))

    def spec(length, offset):
        return pl.BlockSpec((length, head_dim), lambda h: (0, h + offset))

    out_row = pl.BlockSpec((rows, head_dim), lambda h: (0, h))
    out_key = pl.BlockSpec((keys, head_dim), lambda h: (0, h))
    return pl.pallas_call(
        kernel,
        grid=(heads,),
        in_specs=[spec(rows, q_off), spec(keys, k_off), spec(keys, v_off), spec(rows, q_off)],
        out_specs=[out_row, out_row, out_key, out_key],
        out_shape=[
            jax.ShapeDtypeStruct((rows, cols), jnp.float32),
            jax.ShapeDtypeStruct((rows, cols), jnp.float32),
            jax.ShapeDtypeStruct((keys, cols), jnp.bfloat16),
            jax.ShapeDtypeStruct((keys, cols), jnp.bfloat16),
        ],
        compiler_params=pltpu.CompilerParams(vmem_limit_bytes=48 * 1024 * 1024),
        cost_estimate=pl.CostEstimate(
            flops=12 * rows * keys * head_dim * heads,
            transcendentals=rows * keys * heads,
            bytes_accessed=rows * cols * 14 + keys * cols * 8,
        ),
    )(q, k, v, g)


def per_device(
    queries,
    local_keys,
    local_values,
    memory_keys,
    memory_values,
    retrieval,
    gate_logit,
    dropout_keep,
    out_weight,
    cotangent,
):
    mem_count = lax.axis_size("mem")
    mem_index = lax.axis_index("mem")
    tok_rows, feature_cols = queries.shape
    heads_here = gate_logit.shape[0]
    head_dim = feature_cols // heads_here
    blocks_here = memory_keys.shape[0]
    block_len = memory_keys.shape[1]
    query_blocks = tok_rows // QBLK
    top_blocks = retrieval.shape[1]
    request_count = query_blocks * top_blocks
    capacity = 2 * request_count // mem_count
    slot_count = mem_count * capacity
    owner_ids = retrieval // blocks_here
    local_ids = retrieval % blocks_here
    earlier_mask = lax.broadcasted_iota(
        jnp.int32, (request_count, request_count), 0
    ) < lax.broadcasted_iota(jnp.int32, (request_count, request_count), 1)
    same_owner = owner_ids[:, :, None] == owner_ids[:, None, :]
    owner_rank = jnp.sum((same_owner & earlier_mask[None]).astype(jnp.int32), axis=1)
    request_owner = lax.dynamic_index_in_dim(owner_ids, mem_index, 0, keepdims=False)
    request_rank = lax.dynamic_index_in_dim(owner_rank, mem_index, 0, keepdims=False)
    request_slot = ((mem_index - request_owner) % mem_count) * capacity + request_rank
    slot_iota = lax.broadcasted_iota(jnp.int32, (request_count, slot_count), 1)
    pick_table = (request_slot[:, None] == slot_iota).astype(jnp.bfloat16)
    cap_iota = lax.broadcasted_iota(jnp.int32, (mem_count, request_count, capacity), 2)
    wanted = (owner_ids[:, :, None] == mem_index) & (owner_rank[:, :, None] == cap_iota)
    send_local = jnp.sum(wanted.astype(jnp.int32) * (local_ids[:, :, None] + 1), axis=1) - 1
    send_local = jnp.roll(send_local, -mem_index, axis=0)
    block_iota = lax.broadcasted_iota(jnp.int32, (slot_count, blocks_here), 1)
    serve_table = (send_local.reshape(slot_count, 1) == block_iota).astype(jnp.bfloat16)

    gate_values = 1.0 / (1.0 + jnp.exp(-gate_logit))
    gate_cols = jnp.repeat(gate_values, head_dim)[None, :]
    keep_mask = dropout_keep.astype(jnp.float32)

    chunk_heads = heads_here // CHUNKS if heads_here % CHUNKS == 0 else heads_here
    chunk_count = heads_here // chunk_heads
    chunk_cols = chunk_heads * head_dim
    entries2 = block_len * 2 * chunk_cols

    def exchange(buffer, sign):
        pieces = [buffer[0]]
        for shift in range(1, mem_count):
            pairs = [(i, (i + sign * shift) % mem_count) for i in range(mem_count)]
            pieces.append(lax.ppermute(buffer[shift], "mem", pairs))
        return pieces

    def gather_slots(table, pieces):
        total = None
        for shift, piece in enumerate(pieces):
            part = lax.dot_general(
                table[shift * capacity:(shift + 1) * capacity], piece.reshape(capacity, entries2),
                (((0,), (0,)), ((), ())), preferred_element_type=jnp.float32,
            )
            total = part if total is None else total + part
        return total.astype(jnp.bfloat16)

    def fetch(chunk):
        cols = slice(chunk * chunk_cols, (chunk + 1) * chunk_cols)
        both = jnp.concatenate([memory_keys[:, :, cols], memory_values[:, :, cols]], axis=2)
        served = jnp.dot(
            serve_table, both.reshape(blocks_here, entries2), preferred_element_type=jnp.float32
        ).astype(jnp.bfloat16)
        return exchange(served.reshape(mem_count, capacity, block_len, 2 * chunk_cols), 1)

    fetched = [fetch(0)]

    head_count = lax.axis_size("head")
    head_index = lax.axis_index("head")

    def weight_cols(owner):
        return lax.dynamic_slice_in_dim(out_weight, owner * feature_cols, feature_cols, axis=1)

    grad_proj = None
    for shift in range(head_count):
        if shift == 0:
            piece = cotangent
        else:
            pairs = [(i, (i + shift) % head_count) for i in range(head_count)]
            piece = lax.ppermute(cotangent, "head", pairs)
        owner = (head_index - shift) % head_count
        part = lax.dot_general(
            piece, weight_cols(owner), (((1,), (1,)), ((), ())), preferred_element_type=jnp.float32
        )
        grad_proj = part if grad_proj is None else grad_proj + part
    grad_attended = grad_proj * keep_mask * keep_scale
    grad_mem = gate_cols * grad_attended
    grad_loc = (1.0 - gate_cols) * grad_attended

    o_loc, q_loc, k_loc, v_loc = attention_branch(
        queries, grad_loc, local_keys, local_values, heads_here, head_dim, True
    )

    o_mem_parts, q_mem_parts, summed_parts = [], [], []
    for chunk in range(chunk_count):
        if chunk + 1 < chunk_count:
            fetched.append(fetch(chunk + 1))
        chosen = gather_slots(pick_table.T, fetched[chunk]).reshape(
            top_blocks * block_len, 2 * chunk_cols
        )
        o_mem, q_mem, k_mem, v_mem = attention_branch(
            queries, grad_mem, chosen, chosen, chunk_heads, head_dim, False,
            q_off=chunk * chunk_heads, k_off=0, v_off=chunk_heads,
        )
        o_mem_parts.append(o_mem)
        q_mem_parts.append(q_mem)
        parts = jnp.concatenate([k_mem, v_mem], axis=1).reshape(top_blocks, entries2)
        send = lax.dot_general(
            pick_table, parts, (((0,), (0,)), ((), ())), preferred_element_type=jnp.float32
        ).astype(jnp.bfloat16)
        returned = exchange(send.reshape(mem_count, capacity, block_len, 2 * chunk_cols), -1)
        summed_parts.append(
            gather_slots(serve_table, returned).reshape(blocks_here, block_len, 2 * chunk_cols)
        )

    o_mem = jnp.concatenate(o_mem_parts, axis=1)
    q_mem = jnp.concatenate(q_mem_parts, axis=1)
    attended = gate_cols * o_mem + (1.0 - gate_cols) * o_loc
    dropped = (attended * keep_mask * keep_scale).astype(jnp.bfloat16)
    out_sum = None
    for shift in range(head_count):
        target = (head_index + shift) % head_count
        part = jnp.dot(dropped, weight_cols(target), preferred_element_type=jnp.float32)
        if shift:
            pairs = [(i, (i + shift) % head_count) for i in range(head_count)]
            part = lax.ppermute(part, "head", pairs)
        out_sum = part if out_sum is None else out_sum + part
    layer_out = out_sum.astype(jnp.bfloat16)

    grad_queries = (q_mem + q_loc).astype(jnp.bfloat16)
    grad_keys = k_loc
    grad_values = v_loc
    grad_memory_keys = jnp.concatenate([s[:, :, :chunk_cols] for s in summed_parts], axis=2)
    grad_memory_values = jnp.concatenate([s[:, :, chunk_cols:] for s in summed_parts], axis=2)
    return (
        layer_out,
        grad_queries,
        grad_keys,
        grad_values,
        grad_memory_keys,
        grad_memory_values,
    )


def solution(mesh):
    placed = (
        P("mem", "head"),
        P("mem", "head"),
        P("mem", "head"),
        P("mem", None, "head"),
        P("mem", None, "head"),
        P(),
        P("head"),
        P("mem", "head"),
        P("head", None),
        P("mem", "head"),
    )
    return jax.shard_map(
        per_device,
        mesh=mesh,
        in_specs=placed,
        out_specs=(
            P("mem", "head"),
            P("mem", "head"),
            P("mem", "head"),
            P("mem", "head"),
            P("mem", None, "head"),
            P("mem", None, "head"),
        ),
        check_vma=False,
    )
```

```python
import functools

import jax
import jax.numpy as jnp
from jax import lax
from jax.experimental import pallas as pl
from jax.experimental.pallas import tpu as pltpu
from jax.sharding import PartitionSpec as P


QBLK = 512
CHUNKS = 4


keep_scale = 1.0 / 0.9


def _branch_kernel(q_ref, k_ref, v_ref, g_ref, o_ref, dq_ref, dk_ref, dv_ref, *, causal, score_scale):
    q = q_ref[...]
    k = k_ref[...]
    v = v_ref[...]
    g = g_ref[...]
    scores = lax.dot_general(
        q, k, (((1,), (1,)), ((), ())), preferred_element_type=jnp.float32
    ) * score_scale
    if causal:
        row = lax.broadcasted_iota(jnp.int32, scores.shape, 0)
        col = lax.broadcasted_iota(jnp.int32, scores.shape, 1)
        scores = jnp.where(col <= row, scores, -jnp.inf)
    weights = jnp.exp(scores - jnp.max(scores, axis=1, keepdims=True))
    total = jnp.sum(weights, axis=1, keepdims=True)
    mixed = jnp.dot(weights.astype(jnp.bfloat16), v, preferred_element_type=jnp.float32) / total
    o_ref[...] = mixed
    probs = weights / total
    delta = jnp.sum(g * mixed, axis=1, keepdims=True)
    g_low = g.astype(jnp.bfloat16)
    grad_probs = lax.dot_general(
        g_low, v, (((1,), (1,)), ((), ())), preferred_element_type=jnp.float32
    )
    ds = (probs * (grad_probs - delta) * score_scale).astype(jnp.bfloat16)
    dq_ref[...] = jnp.dot(ds, k, preferred_element_type=jnp.float32)
    dk_ref[...] = lax.dot_general(
        ds, q, (((0,), (0,)), ((), ())), preferred_element_type=jnp.float32
    ).astype(dk_ref.dtype)
    dv_ref[...] = lax.dot_general(
        probs.astype(jnp.bfloat16), g_low, (((0,), (0,)), ((), ())),
        preferred_element_type=jnp.float32,
    ).astype(dv_ref.dtype)


def attention_branch(q, g, k, v, heads, head_dim, causal, q_off=0, k_off=0, v_off=0):
    rows = q.shape[0]
    keys = k.shape[0]
    cols = heads * head_dim
    kernel = functools.partial(_branch_kernel, causal=causal, score_scale=head_dim ** (-0.5))

    def spec(length, offset):
        return pl.BlockSpec((length, head_dim), lambda h: (0, h + offset))

    out_row = pl.BlockSpec((rows, head_dim), lambda h: (0, h))
    out_key = pl.BlockSpec((keys, head_dim), lambda h: (0, h))
    return pl.pallas_call(
        kernel,
        grid=(heads,),
        in_specs=[spec(rows, q_off), spec(keys, k_off), spec(keys, v_off), spec(rows, q_off)],
        out_specs=[out_row, out_row, out_key, out_key],
        out_shape=[
            jax.ShapeDtypeStruct((rows, cols), jnp.float32),
            jax.ShapeDtypeStruct((rows, cols), jnp.float32),
            jax.ShapeDtypeStruct((keys, cols), jnp.bfloat16),
            jax.ShapeDtypeStruct((keys, cols), jnp.bfloat16),
        ],
        compiler_params=pltpu.CompilerParams(vmem_limit_bytes=48 * 1024 * 1024),
        cost_estimate=pl.CostEstimate(
            flops=12 * rows * keys * head_dim * heads,
            transcendentals=rows * keys * heads,
            bytes_accessed=rows * cols * 14 + keys * cols * 8,
        ),
    )(q, k, v, g)


def _gather_kernel(*refs):
    table_ref = refs[0]
    pieces = refs[1:-1]
    out_ref = refs[-1]
    capacity = pieces[0].shape[0]
    total = None
    for shift, piece in enumerate(pieces):
        rows = table_ref[shift * capacity:(shift + 1) * capacity, :].astype(jnp.bfloat16)
        part = lax.dot_general(rows, piece[...], (((0,), (0,)), ((), ())), preferred_element_type=jnp.float32)
        total = part if total is None else total + part
    out_ref[...] = total.astype(out_ref.dtype)


def gather_pieces(table, pieces):
    out_rows = table.shape[1]
    capacity, entries = pieces[0].shape
    whole = pl.BlockSpec(memory_space=pltpu.VMEM)
    return pl.pallas_call(
        _gather_kernel,
        in_specs=[whole] * (1 + len(pieces)),
        out_specs=whole,
        out_shape=jax.ShapeDtypeStruct((out_rows, entries), jnp.bfloat16),
        compiler_params=pltpu.CompilerParams(vmem_limit_bytes=32 * 1024 * 1024),
        cost_estimate=pl.CostEstimate(
            flops=2 * table.shape[0] * out_rows * entries, transcendentals=0,
            bytes_accessed=len(pieces) * capacity * entries * 2 + out_rows * entries * 2,
        ),
    )(table, *pieces)


def per_device(
    queries,
    local_keys,
    local_values,
    memory_keys,
    memory_values,
    retrieval,
    gate_logit,
    dropout_keep,
    out_weight,
    cotangent,
):
    mem_count = lax.axis_size("mem")
    mem_index = lax.axis_index("mem")
    tok_rows, feature_cols = queries.shape
    heads_here = gate_logit.shape[0]
    head_dim = feature_cols // heads_here
    blocks_here = memory_keys.shape[0]
    block_len = memory_keys.shape[1]
    query_blocks = tok_rows // QBLK
    top_blocks = retrieval.shape[1]
    request_count = query_blocks * top_blocks
    capacity = 2 * request_count // mem_count
    slot_count = mem_count * capacity
    owner_ids = retrieval // blocks_here
    local_ids = retrieval % blocks_here
    earlier_mask = lax.broadcasted_iota(
        jnp.int32, (request_count, request_count), 0
    ) < lax.broadcasted_iota(jnp.int32, (request_count, request_count), 1)
    same_owner = owner_ids[:, :, None] == owner_ids[:, None, :]
    owner_rank = jnp.sum((same_owner & earlier_mask[None]).astype(jnp.int32), axis=1)
    request_owner = lax.dynamic_index_in_dim(owner_ids, mem_index, 0, keepdims=False)
    request_rank = lax.dynamic_index_in_dim(owner_rank, mem_index, 0, keepdims=False)
    request_slot = ((mem_index - request_owner) % mem_count) * capacity + request_rank
    slot_iota = lax.broadcasted_iota(jnp.int32, (request_count, slot_count), 1)
    pick_table = (request_slot[:, None] == slot_iota).astype(jnp.bfloat16)
    cap_iota = lax.broadcasted_iota(jnp.int32, (mem_count, request_count, capacity), 2)
    wanted = (owner_ids[:, :, None] == mem_index) & (owner_rank[:, :, None] == cap_iota)
    send_local = jnp.sum(wanted.astype(jnp.int32) * (local_ids[:, :, None] + 1), axis=1) - 1
    send_local = jnp.roll(send_local, -mem_index, axis=0)
    block_iota = lax.broadcasted_iota(jnp.int32, (slot_count, blocks_here), 1)
    serve_table = (send_local.reshape(slot_count, 1) == block_iota).astype(jnp.bfloat16)

    gate_values = 1.0 / (1.0 + jnp.exp(-gate_logit))
    gate_cols = jnp.repeat(gate_values, head_dim)[None, :]
    keep_mask = dropout_keep.astype(jnp.float32)

    chunk_heads = max(1, heads_here // CHUNKS)
    chunk_count = heads_here // chunk_heads
    chunk_cols = chunk_heads * head_dim
    entries2 = block_len * 2 * chunk_cols

    def exchange(buffer, sign):
        pieces = [buffer[0]]
        for shift in range(1, mem_count):
            pairs = [(i, (i + sign * shift) % mem_count) for i in range(mem_count)]
            pieces.append(lax.ppermute(buffer[shift], "mem", pairs))
        return pieces

    def gather_slots(table, pieces):
        return gather_pieces(
            table.astype(jnp.float32), [piece.reshape(capacity, entries2) for piece in pieces]
        )

    def fetch(chunk):
        cols = slice(chunk * chunk_cols, (chunk + 1) * chunk_cols)
        both = jnp.concatenate([memory_keys[:, :, cols], memory_values[:, :, cols]], axis=2)
        served = jnp.dot(
            serve_table, both.reshape(blocks_here, entries2), preferred_element_type=jnp.float32
        ).astype(jnp.bfloat16)
        return exchange(served.reshape(mem_count, capacity, block_len, 2 * chunk_cols), 1)

    fetched = [fetch(0)]

    head_count = lax.axis_size("head")
    head_index = lax.axis_index("head")

    def weight_cols(owner):
        return lax.dynamic_slice_in_dim(out_weight, owner * feature_cols, feature_cols, axis=1)

    grad_proj = None
    for shift in range(head_count):
        if shift == 0:
            piece = cotangent
        else:
            pairs = [(i, (i + shift) % head_count) for i in range(head_count)]
            piece = lax.ppermute(cotangent, "head", pairs)
        owner = (head_index - shift) % head_count
        part = lax.dot_general(
            piece, weight_cols(owner), (((1,), (1,)), ((), ())), preferred_element_type=jnp.float32
        )
        grad_proj = part if grad_proj is None else grad_proj + part
    grad_attended = grad_proj * keep_mask * keep_scale
    grad_mem = gate_cols * grad_attended
    grad_loc = (1.0 - gate_cols) * grad_attended

    o_loc, q_loc, k_loc, v_loc = attention_branch(
        queries, grad_loc, local_keys, local_values, heads_here, head_dim, True
    )

    if chunk_count > 1:
        memory_keys, memory_values, o_loc, q_loc, k_loc, v_loc, grad_mem = lax.optimization_barrier(
            (memory_keys, memory_values, o_loc, q_loc, k_loc, v_loc, grad_mem)
        )
    o_mem_parts, q_mem_parts, summed_parts = [], [], []
    for chunk in range(chunk_count):
        if chunk + 1 < chunk_count:
            fetched.append(fetch(chunk + 1))
        chosen = gather_slots(pick_table.T, fetched[chunk]).reshape(
            top_blocks * block_len, 2 * chunk_cols
        )
        o_mem, q_mem, k_mem, v_mem = attention_branch(
            queries, grad_mem, chosen, chosen, chunk_heads, head_dim, False,
            q_off=chunk * chunk_heads, k_off=0, v_off=chunk_heads,
        )
        o_mem_parts.append(o_mem)
        q_mem_parts.append(q_mem)
        parts = jnp.concatenate([k_mem, v_mem], axis=1).reshape(top_blocks, entries2)
        send = lax.dot_general(
            pick_table, parts, (((0,), (0,)), ((), ())), preferred_element_type=jnp.float32
        ).astype(jnp.bfloat16)
        if chunk + 1 < chunk_count:
            send, fetched[chunk + 1] = lax.optimization_barrier((send, fetched[chunk + 1]))
        returned = exchange(send.reshape(mem_count, capacity, block_len, 2 * chunk_cols), -1)
        summed_parts.append(
            gather_slots(serve_table, returned).reshape(blocks_here, block_len, 2 * chunk_cols)
        )

    o_mem = jnp.concatenate(o_mem_parts, axis=1)
    q_mem = jnp.concatenate(q_mem_parts, axis=1)
    attended = gate_cols * o_mem + (1.0 - gate_cols) * o_loc
    dropped = (attended * keep_mask * keep_scale).astype(jnp.bfloat16)
    out_sum = None
    for shift in range(head_count):
        target = (head_index + shift) % head_count
        part = jnp.dot(dropped, weight_cols(target), preferred_element_type=jnp.float32)
        if shift:
            pairs = [(i, (i + shift) % head_count) for i in range(head_count)]
            part = lax.ppermute(part, "head", pairs)
        out_sum = part if out_sum is None else out_sum + part
    layer_out = out_sum.astype(jnp.bfloat16)

    grad_queries = (q_mem + q_loc).astype(jnp.bfloat16)
    grad_keys = k_loc
    grad_values = v_loc
    grad_memory_keys = jnp.concatenate([s[:, :, :chunk_cols] for s in summed_parts], axis=2)
    grad_memory_values = jnp.concatenate([s[:, :, chunk_cols:] for s in summed_parts], axis=2)
    return (
        layer_out,
        grad_queries,
        grad_keys,
        grad_values,
        grad_memory_keys,
        grad_memory_values,
    )


def solution(mesh):
    placed = (
        P("mem", "head"),
        P("mem", "head"),
        P("mem", "head"),
        P("mem", None, "head"),
        P("mem", None, "head"),
        P(),
        P("head"),
        P("mem", "head"),
        P("head", None),
        P("mem", "head"),
    )
    return jax.shard_map(
        per_device,
        mesh=mesh,
        in_specs=placed,
        out_specs=(
            P("mem", "head"),
            P("mem", "head"),
            P("mem", "head"),
            P("mem", "head"),
            P("mem", None, "head"),
            P("mem", None, "head"),
        ),
        check_vma=False,
    )
```

```python
import functools

import jax
import jax.numpy as jnp
from jax import lax
from jax.experimental import pallas as pl
from jax.experimental.pallas import tpu as pltpu
from jax.sharding import PartitionSpec as P


QBLK = 512
CHUNKS = 2


keep_scale = 1.0 / 0.9


def _branch_kernel(q_ref, k_ref, v_ref, g_ref, o_ref, dq_ref, dk_ref, dv_ref, *, causal, score_scale):
    q = q_ref[...]
    k = k_ref[...]
    v = v_ref[...]
    g = g_ref[...]
    scores = lax.dot_general(
        q, k, (((1,), (1,)), ((), ())), preferred_element_type=jnp.float32
    ) * score_scale
    if causal:
        row = lax.broadcasted_iota(jnp.int32, scores.shape, 0)
        col = lax.broadcasted_iota(jnp.int32, scores.shape, 1)
        scores = jnp.where(col <= row, scores, -jnp.inf)
    weights = jnp.exp(scores - jnp.max(scores, axis=1, keepdims=True))
    total = jnp.sum(weights, axis=1, keepdims=True)
    mixed = jnp.dot(weights.astype(jnp.bfloat16), v, preferred_element_type=jnp.float32) / total
    o_ref[...] = mixed
    probs = weights / total
    delta = jnp.sum(g * mixed, axis=1, keepdims=True)
    g_low = g.astype(jnp.bfloat16)
    grad_probs = lax.dot_general(
        g_low, v, (((1,), (1,)), ((), ())), preferred_element_type=jnp.float32
    )
    ds = (probs * (grad_probs - delta) * score_scale).astype(jnp.bfloat16)
    dq_ref[...] = jnp.dot(ds, k, preferred_element_type=jnp.float32)
    dk_ref[...] = lax.dot_general(
        ds, q, (((0,), (0,)), ((), ())), preferred_element_type=jnp.float32
    ).astype(dk_ref.dtype)
    dv_ref[...] = lax.dot_general(
        probs.astype(jnp.bfloat16), g_low, (((0,), (0,)), ((), ())),
        preferred_element_type=jnp.float32,
    ).astype(dv_ref.dtype)


def attention_branch(q, g, k, v, heads, head_dim, causal, q_off=0, k_off=0, v_off=0):
    rows = q.shape[0]
    keys = k.shape[0]
    cols = heads * head_dim
    kernel = functools.partial(_branch_kernel, causal=causal, score_scale=head_dim ** (-0.5))

    def spec(length, offset):
        return pl.BlockSpec((length, head_dim), lambda h: (0, h + offset))

    out_row = pl.BlockSpec((rows, head_dim), lambda h: (0, h))
    out_key = pl.BlockSpec((keys, head_dim), lambda h: (0, h))
    return pl.pallas_call(
        kernel,
        grid=(heads,),
        in_specs=[spec(rows, q_off), spec(keys, k_off), spec(keys, v_off), spec(rows, q_off)],
        out_specs=[out_row, out_row, out_key, out_key],
        out_shape=[
            jax.ShapeDtypeStruct((rows, cols), jnp.float32),
            jax.ShapeDtypeStruct((rows, cols), jnp.float32),
            jax.ShapeDtypeStruct((keys, cols), jnp.bfloat16),
            jax.ShapeDtypeStruct((keys, cols), jnp.bfloat16),
        ],
        compiler_params=pltpu.CompilerParams(vmem_limit_bytes=48 * 1024 * 1024),
        cost_estimate=pl.CostEstimate(
            flops=12 * rows * keys * head_dim * heads,
            transcendentals=rows * keys * heads,
            bytes_accessed=rows * cols * 14 + keys * cols * 8,
        ),
    )(q, k, v, g)


def _gather_kernel(*refs):
    table_ref = refs[0]
    pieces = refs[1:-1]
    out_ref = refs[-1]
    capacity = pieces[0].shape[0]
    total = None
    for shift, piece in enumerate(pieces):
        rows = table_ref[shift * capacity:(shift + 1) * capacity, :].astype(jnp.bfloat16)
        part = lax.dot_general(rows, piece[...], (((0,), (0,)), ((), ())), preferred_element_type=jnp.float32)
        total = part if total is None else total + part
    out_ref[...] = total.astype(out_ref.dtype)


def gather_pieces(table, pieces):
    out_rows = table.shape[1]
    capacity, entries = pieces[0].shape
    whole = pl.BlockSpec(memory_space=pltpu.VMEM)
    return pl.pallas_call(
        _gather_kernel,
        in_specs=[whole] * (1 + len(pieces)),
        out_specs=whole,
        out_shape=jax.ShapeDtypeStruct((out_rows, entries), jnp.bfloat16),
        compiler_params=pltpu.CompilerParams(vmem_limit_bytes=32 * 1024 * 1024),
        cost_estimate=pl.CostEstimate(
            flops=2 * table.shape[0] * out_rows * entries, transcendentals=0,
            bytes_accessed=len(pieces) * capacity * entries * 2 + out_rows * entries * 2,
        ),
    )(table, *pieces)


def per_device(
    queries,
    local_keys,
    local_values,
    memory_keys,
    memory_values,
    retrieval,
    gate_logit,
    dropout_keep,
    out_weight,
    cotangent,
):
    mem_count = lax.axis_size("mem")
    mem_index = lax.axis_index("mem")
    tok_rows, feature_cols = queries.shape
    heads_here = gate_logit.shape[0]
    head_dim = feature_cols // heads_here
    blocks_here = memory_keys.shape[0]
    block_len = memory_keys.shape[1]
    query_blocks = tok_rows // QBLK
    top_blocks = retrieval.shape[1]
    request_count = query_blocks * top_blocks
    capacity = 2 * request_count // mem_count
    slot_count = mem_count * capacity
    owner_ids = retrieval // blocks_here
    local_ids = retrieval % blocks_here
    earlier_mask = lax.broadcasted_iota(
        jnp.int32, (request_count, request_count), 0
    ) < lax.broadcasted_iota(jnp.int32, (request_count, request_count), 1)
    same_owner = owner_ids[:, :, None] == owner_ids[:, None, :]
    owner_rank = jnp.sum((same_owner & earlier_mask[None]).astype(jnp.int32), axis=1)
    request_owner = lax.dynamic_index_in_dim(owner_ids, mem_index, 0, keepdims=False)
    request_rank = lax.dynamic_index_in_dim(owner_rank, mem_index, 0, keepdims=False)
    request_slot = ((mem_index - request_owner) % mem_count) * capacity + request_rank
    slot_iota = lax.broadcasted_iota(jnp.int32, (request_count, slot_count), 1)
    pick_table = (request_slot[:, None] == slot_iota).astype(jnp.bfloat16)
    cap_iota = lax.broadcasted_iota(jnp.int32, (mem_count, request_count, capacity), 2)
    wanted = (owner_ids[:, :, None] == mem_index) & (owner_rank[:, :, None] == cap_iota)
    send_local = jnp.sum(wanted.astype(jnp.int32) * (local_ids[:, :, None] + 1), axis=1) - 1
    send_local = jnp.roll(send_local, -mem_index, axis=0)
    block_iota = lax.broadcasted_iota(jnp.int32, (slot_count, blocks_here), 1)
    serve_table = (send_local.reshape(slot_count, 1) == block_iota).astype(jnp.bfloat16)

    gate_values = 1.0 / (1.0 + jnp.exp(-gate_logit))
    gate_cols = jnp.repeat(gate_values, head_dim)[None, :]
    keep_mask = dropout_keep.astype(jnp.float32)

    chunk_heads = heads_here // CHUNKS if heads_here % CHUNKS == 0 else heads_here
    chunk_count = heads_here // chunk_heads
    chunk_cols = chunk_heads * head_dim
    entries2 = block_len * 2 * chunk_cols

    def exchange(buffer, sign):
        pieces = [buffer[0]]
        for shift in range(1, mem_count):
            pairs = [(i, (i + sign * shift) % mem_count) for i in range(mem_count)]
            pieces.append(lax.ppermute(buffer[shift], "mem", pairs))
        return pieces

    def gather_slots(table, pieces):
        return gather_pieces(
            table.astype(jnp.float32), [piece.reshape(capacity, entries2) for piece in pieces]
        )

    def fetch(chunk):
        cols = slice(chunk * chunk_cols, (chunk + 1) * chunk_cols)
        both = jnp.concatenate([memory_keys[:, :, cols], memory_values[:, :, cols]], axis=2)
        served = jnp.dot(
            serve_table, both.reshape(blocks_here, entries2), preferred_element_type=jnp.float32
        ).astype(jnp.bfloat16)
        return exchange(served.reshape(mem_count, capacity, block_len, 2 * chunk_cols), 1)

    fetched = [fetch(0)]

    head_count = lax.axis_size("head")
    head_index = lax.axis_index("head")

    def weight_cols(owner):
        return lax.dynamic_slice_in_dim(out_weight, owner * feature_cols, feature_cols, axis=1)

    grad_proj = None
    for shift in range(head_count):
        if shift == 0:
            piece = cotangent
        else:
            pairs = [(i, (i + shift) % head_count) for i in range(head_count)]
            piece = lax.ppermute(cotangent, "head", pairs)
        owner = (head_index - shift) % head_count
        part = lax.dot_general(
            piece, weight_cols(owner), (((1,), (1,)), ((), ())), preferred_element_type=jnp.float32
        )
        grad_proj = part if grad_proj is None else grad_proj + part
    grad_attended = grad_proj * keep_mask * keep_scale
    grad_mem = gate_cols * grad_attended
    grad_loc = (1.0 - gate_cols) * grad_attended

    o_loc, q_loc, k_loc, v_loc = attention_branch(
        queries, grad_loc, local_keys, local_values, heads_here, head_dim, True
    )

    o_mem_parts, q_mem_parts, summed_parts = [], [], []
    for chunk in range(chunk_count):
        if chunk + 1 < chunk_count:
            fetched.append(fetch(chunk + 1))
        chosen = gather_slots(pick_table.T, fetched[chunk]).reshape(
            top_blocks * block_len, 2 * chunk_cols
        )
        o_mem, q_mem, k_mem, v_mem = attention_branch(
            queries, grad_mem, chosen, chosen, chunk_heads, head_dim, False,
            q_off=chunk * chunk_heads, k_off=0, v_off=chunk_heads,
        )
        o_mem_parts.append(o_mem)
        q_mem_parts.append(q_mem)
        parts = jnp.concatenate([k_mem, v_mem], axis=1).reshape(top_blocks, entries2)
        send = lax.dot_general(
            pick_table, parts, (((0,), (0,)), ((), ())), preferred_element_type=jnp.float32
        ).astype(jnp.bfloat16)
        if chunk + 1 < chunk_count:
            send, fetched[chunk + 1] = lax.optimization_barrier((send, fetched[chunk + 1]))
        returned = exchange(send.reshape(mem_count, capacity, block_len, 2 * chunk_cols), -1)
        summed_parts.append(
            gather_slots(serve_table, returned).reshape(blocks_here, block_len, 2 * chunk_cols)
        )

    o_mem = jnp.concatenate(o_mem_parts, axis=1)
    q_mem = jnp.concatenate(q_mem_parts, axis=1)
    attended = gate_cols * o_mem + (1.0 - gate_cols) * o_loc
    dropped = (attended * keep_mask * keep_scale).astype(jnp.bfloat16)
    out_sum = None
    for shift in range(head_count):
        target = (head_index + shift) % head_count
        part = jnp.dot(dropped, weight_cols(target), preferred_element_type=jnp.float32)
        if shift:
            pairs = [(i, (i + shift) % head_count) for i in range(head_count)]
            part = lax.ppermute(part, "head", pairs)
        out_sum = part if out_sum is None else out_sum + part
    layer_out = out_sum.astype(jnp.bfloat16)

    grad_queries = (q_mem + q_loc).astype(jnp.bfloat16)
    grad_keys = k_loc
    grad_values = v_loc
    grad_memory_keys = jnp.concatenate([s[:, :, :chunk_cols] for s in summed_parts], axis=2)
    grad_memory_values = jnp.concatenate([s[:, :, chunk_cols:] for s in summed_parts], axis=2)
    return (
        layer_out,
        grad_queries,
        grad_keys,
        grad_values,
        grad_memory_keys,
        grad_memory_values,
    )


def solution(mesh):
    placed = (
        P("mem", "head"),
        P("mem", "head"),
        P("mem", "head"),
        P("mem", None, "head"),
        P("mem", None, "head"),
        P(),
        P("head"),
        P("mem", "head"),
        P("head", None),
        P("mem", "head"),
    )
    return jax.shard_map(
        per_device,
        mesh=mesh,
        in_specs=placed,
        out_specs=(
            P("mem", "head"),
            P("mem", "head"),
            P("mem", "head"),
            P("mem", "head"),
            P("mem", None, "head"),
            P("mem", None, "head"),
        ),
        check_vma=False,
    )
```
